128 devices in a mesh: dp: 128 (over x, y, z, core).
Axes of the slice: x: 4, y: 4, z: 4, core: 2. Of those that a mesh axis runs over, the one named last changes fastest.
Arguments:
- hidden_in: bfloat16 [32768, 4096], P('dp'), may hold values from -24 to 24
- queries: bfloat16 [32768, 2048], P('dp'), may hold values from -16 to 16
- keys: bfloat16 [32768, 512], P('dp'), may hold values from -16 to 16
- values: bfloat16 [32768, 512], P('dp'), may hold values from -6 to 6
- grad_attn: bfloat16 [32768, 2048], P('dp'), may hold values from -6 to 6
- send_rows: int32 [4, 128], replicated, may hold values from -1 to 255, as said below
- slot_docs: int32 [128, 4], P('dp'), may hold values from -1 to 255, as said below
Outputs:
- grad_queries: bfloat16 [32768, 2048], P('dp')
- grad_keys: bfloat16 [32768, 512], P('dp')
- grad_values: bfloat16 [32768, 512], P('dp')
- grad_wv: float32 [4096, 512], P('dp')
The draws below stay inside these ranges and needn't reach their ends.
Inputs may be any that keep to these rules, and one draw needn't show every extreme that they name: `send_rows`: every owner sends the same local rows to a rank. Each local row appears exactly once. The rows sent to one rank form whole documents at consecutive slots, the local rows of a document consecutive and rising with the slot; a document has at most 4 local rows, and in every draw some rank has all 4 slots used. slot_docs[r, j] is -1 exactly where send_rows[j, r] is -1; slots with the same number hold one document, and distinct documents have distinct numbers.
All inputs are finite; a program needn't handle non-finite values.
Results may differ from the reference program's by a relative error of at most 0.0057.
Values may be sent and summed in bfloat16 or wider, within the bound.
No kernel may reach another device: no remote copies, remote signals or barrier semaphores. Data moves between devices by JAX's collectives and lax.ppermute only.
A program may use at most 128 MiB of HBM per device.

```python
import math
import jax
import jax.numpy as jnp
from jax import lax

D = 4096
HQ = 16
HK = 4
DH = 128
MOST = 4
TOK_DEV = 256
TOKENS = 32768


def doc_layout(key):
    owners = TOKENS // TOK_DEV
    doc_lens = jax.random.randint(jax.random.fold_in(key, 11), (TOK_DEV,), 1, MOST + 1, dtype=jnp.int32)
    doc_lens = doc_lens.at[0].set(MOST)
    doc_ends = jnp.cumsum(doc_lens)
    doc_starts = doc_ends - doc_lens
    exists = doc_starts < TOK_DEV
    doc_lens = jnp.where(exists, jnp.minimum(doc_lens, TOK_DEV - doc_starts), 0).astype(jnp.int32)
    doc_cost = doc_lens * doc_lens
    doc_order = jnp.argsort(-doc_cost, stable=True).astype(jnp.int32)
    ranks = jnp.arange(owners, dtype=jnp.int32)

    def place_doc(state_pair, doc_index):
        rank_load, rank_used = state_pair
        doc_size = doc_lens[doc_index]
        can_fit = rank_used + doc_size <= MOST
        rank_score = jnp.where(can_fit, rank_load * owners + ranks, 2 ** 30)
        chosen = jnp.argmin(rank_score).astype(jnp.int32)
        first_slot = rank_used[chosen]
        to_grow = (ranks == chosen) & (doc_size > 0)
        rank_load = rank_load + jnp.where(to_grow, doc_size * doc_size, 0)
        rank_used = rank_used + jnp.where(to_grow, doc_size, 0)
        return ((rank_load, rank_used), (chosen, first_slot))
    start_pair = (jnp.zeros((owners,), jnp.int32), jnp.zeros((owners,), jnp.int32))
    unused, (chosen_ranks, first_slots) = lax.scan(place_doc, start_pair, doc_order)
    doc_dest = jnp.zeros((TOK_DEV,), jnp.int32).at[doc_order].set(chosen_ranks)
    doc_slot = jnp.zeros((TOK_DEV,), jnp.int32).at[doc_order].set(first_slots)
    start_marks = jnp.zeros((TOK_DEV,), jnp.int32).at[jnp.where(exists, doc_starts, TOK_DEV)].add(1, mode='drop')
    doc_of = jnp.cumsum(start_marks) - 1
    local_rows = jnp.arange(TOK_DEV, dtype=jnp.int32)
    rank_of = doc_dest[doc_of]
    slot_of = doc_slot[doc_of] + local_rows - doc_starts[doc_of]
    doc_number = (doc_starts + doc_lens - 1).astype(jnp.int32)[doc_of]
    send_list = jnp.full((MOST, owners), -1, jnp.int32).at[slot_of, rank_of].set(local_rows)
    doc_list = jnp.full((owners, MOST), -1, jnp.int32).at[rank_of, slot_of].set(doc_number.astype(jnp.int32))
    return (send_list, doc_list)


def draw_send_rows(key, part):
    return doc_layout(key)[0]


def draw_slot_docs(key, part):
    return doc_layout(key)[1]


def draw_queries(key, part):
    drawn = jax.random.truncated_normal(jax.random.fold_in(key, 81), -6.0, 6.0, (TOKENS, HQ * DH), jnp.float32)
    return drawn.astype(jnp.bfloat16)


def draw_keys(key, part):
    drawn = jax.random.truncated_normal(jax.random.fold_in(key, 91), -6.0, 6.0, (TOKENS, HK * DH), jnp.float32)
    return drawn.astype(jnp.bfloat16)


def with_spikes(values, stream_key, source, target, parts, factor):
    def block_of(axis_at):
        return (jnp.arange(values.shape[axis_at]) // (values.shape[axis_at] // parts)).reshape((-1,) + (1,) * (values.ndim - 1 - axis_at))

    first = jax.random.permutation(stream_key, parts)[block_of(target)]
    second = (block_of(target) + parts // 2) % parts
    return jnp.where((block_of(source) == first) | (block_of(source) == second), factor * values, values)


def steps_of(key, shape, pieces, smallest, high):
    factor_of = 1.0
    for axis_at, parts in pieces:
        heights = jax.random.uniform(jax.random.fold_in(jax.random.fold_in(key, 6), axis_at), (parts,), jnp.float32, smallest / len(pieces), high / len(pieces))
        factor_of = factor_of * jnp.repeat(jnp.exp(heights), shape[axis_at] // parts).reshape((-1,) + (1,) * (len(shape) - 1 - axis_at))
    return factor_of


def scatter_about(own_key, dims, scale, reach, split=(), held_as=jnp.bfloat16):
    level = steps_of(own_key, dims, split, -0.22, 0.18) if split else 1.0
    values = jax.random.normal(own_key, dims, jnp.float32) * scale * level
    return jnp.minimum(jnp.maximum(values, -reach), reach).astype(held_as)


def bell_draw_with(stream_key, extent, deviation, most, split, heavy, held_as=jnp.bfloat16):
    result = deviation * jax.random.normal(stream_key, extent, jnp.float32)
    if split:
        result = result * steps_of(stream_key, extent, split, -0.22, 0.18)
    return jnp.clip(with_spikes(result, jax.random.fold_in(stream_key, 3), *heavy), -most, most).astype(held_as)


def setup_inputs(seed: int = 0) -> dict:
    streams_of = jax.random.split(jax.random.key(seed), 8)
    return {
        "hidden_in": bell_draw_with(streams_of[0], (TOKENS, D), 1.0, 24.0, ((0, 128),), (0, 1, 128, 5.5)),
        "queries": draw_queries(jax.random.fold_in(streams_of[7], 71), 0),
        "keys": draw_keys(jax.random.fold_in(streams_of[7], 71), 0),
        "values": scatter_about(streams_of[3], (TOKENS, HK * DH), 1.0, 6.0, ((0, 128),)),
        "grad_attn": scatter_about(streams_of[4], (TOKENS, HQ * DH), 1.0, 6.0, ((0, 128),)),
        "send_rows": draw_send_rows(jax.random.fold_in(streams_of[7], 71), 0),
        "slot_docs": draw_slot_docs(jax.random.fold_in(streams_of[7], 71), 0),
    }


def attend_rows(q_rows, k_rows, v_rows, o_rows, segment):
    row_count = q_rows.shape[0]
    group_size = HQ // HK
    score_scale = 1.0 / math.sqrt(DH)
    order_ids = jnp.arange(row_count, dtype=jnp.int32)
    live_rows = segment >= 0
    allowed = (segment[:, None] == segment[None, :]) & (order_ids[None, :] <= order_ids[:, None]) & live_rows[:, None]
    q_four = q_rows.astype(jnp.float32).reshape(row_count, HK, group_size, DH)
    o_four = o_rows.astype(jnp.float32).reshape(row_count, HK, group_size, DH)
    k_three = k_rows.astype(jnp.float32).reshape(row_count, HK, DH)
    v_three = v_rows.astype(jnp.float32).reshape(row_count, HK, DH)
    grad_q_list = []
    grad_k_list = []
    grad_v_list = []
    for head_kv in range(HK):
        q_group = q_four[:, head_kv]
        o_group = o_four[:, head_kv]
        k_group = k_three[:, head_kv]
        v_group = v_three[:, head_kv]
        scores = jnp.einsum('qhd,kd->hqk', q_group, k_group) * score_scale
        scores = jnp.where(allowed[None], scores, jnp.float32(-1000000000.0))
        row_max = lax.optimization_barrier(jnp.max(scores, axis=-1, keepdims=True))
        weights = jnp.exp(scores - row_max)
        attn_probs = weights / lax.optimization_barrier(jnp.sum(weights, axis=-1, keepdims=True))
        attn_probs = jnp.where(live_rows[None, :, None], attn_probs, jnp.float32(0.0))
        probs_b = lax.optimization_barrier(attn_probs.astype(jnp.bfloat16)).astype(jnp.float32)
        grad_v_list.append(jnp.einsum('hqk,qhd->kd', probs_b, o_group))
        dprob = jnp.einsum('qhd,kd->hqk', o_group, v_group)
        row_delta = lax.optimization_barrier(jnp.sum(attn_probs * dprob, axis=-1, keepdims=True))
        dscore = lax.optimization_barrier((attn_probs * (dprob - row_delta) * score_scale).astype(jnp.bfloat16)).astype(jnp.float32)
        grad_q_list.append(jnp.einsum('hqk,kd->qhd', dscore, k_group))
        grad_k_list.append(jnp.einsum('hqk,qhd->kd', dscore, q_group))
    grad_q_rows = jnp.stack(grad_q_list, axis=1).reshape(row_count, HQ * DH).astype(jnp.bfloat16)
    grad_k_rows = jnp.stack(grad_k_list, axis=1).reshape(row_count, HK * DH).astype(jnp.bfloat16)
    grad_v_rows = jnp.stack(grad_v_list, axis=1).reshape(row_count, HK * DH).astype(jnp.bfloat16)
    return (grad_q_rows, grad_k_rows, grad_v_rows)

def reference(hidden_in, queries, keys, values, grad_attn, send_rows, slot_docs):
    owners = TOKENS // TOK_DEV

    def per_rank(outputs, rank):
        local_rows = send_rows[:, rank]
        live_slots = local_rows >= 0
        global_rows = (jnp.arange(owners, dtype=jnp.int32)[None, :] * TOK_DEV + jnp.maximum(local_rows, 0)[:, None]).reshape(-1).astype(jnp.int32)
        segment = jnp.broadcast_to(slot_docs[rank][:, None], (MOST, owners)).reshape(-1)
        results = attend_rows(queries[global_rows], keys[global_rows], values[global_rows], grad_attn[global_rows], segment)
        live_rows = jnp.broadcast_to(live_slots[:, None], (MOST, owners)).reshape(-1)
        targets = jnp.where(live_rows, global_rows, TOKENS).astype(jnp.int32)
        updated = tuple((whole.at[targets].set(part_rows, mode='drop') for whole, part_rows in zip(outputs, results)))
        return (updated, None)
    initial = (jnp.zeros((TOKENS, HQ * DH), jnp.bfloat16), jnp.zeros((TOKENS, HK * DH), jnp.bfloat16), jnp.zeros((TOKENS, HK * DH), jnp.bfloat16))
    outputs, unused = lax.scan(per_rank, initial, jnp.arange(owners, dtype=jnp.int32))
    grad_queries, grad_keys, grad_values = outputs
    grad_wv = jnp.dot(hidden_in.T, grad_values, preferred_element_type=jnp.float32) * (1.0 / math.sqrt(TOKENS))
    return (grad_queries, grad_keys, grad_values, grad_wv)
```

```python
import math

import jax
import jax.numpy as jnp
from jax import lax
from jax.sharding import PartitionSpec as P

HQ = 16
HK = 4
DH = 128


def attend_rows(q_rows, k_rows, v_rows, o_rows, segment):
    row_count = q_rows.shape[0]
    group_size = HQ // HK
    score_scale = 1.0 / math.sqrt(DH)
    order_ids = jnp.arange(row_count, dtype=jnp.int32)
    live_rows = segment >= 0
    allowed = (
        (segment[:, None] == segment[None, :])
        & (order_ids[None, :] <= order_ids[:, None])
        & live_rows[:, None]
    )
    q_four = q_rows.reshape(row_count, HK, group_size, DH)
    o_four = o_rows.reshape(row_count, HK, group_size, DH)
    k_three = k_rows.reshape(row_count, HK, DH)
    v_three = v_rows.reshape(row_count, HK, DH)
    grad_q_list = []
    grad_k_list = []
    grad_v_list = []
    for head_kv in range(HK):
        q_group = q_four[:, head_kv]
        o_group = o_four[:, head_kv]
        k_group = k_three[:, head_kv]
        v_group = v_three[:, head_kv]
        scores = (
            jnp.einsum("qhd,kd->hqk", q_group, k_group, preferred_element_type=jnp.float32)
            * score_scale
        )
        scores = jnp.where(allowed[None], scores, jnp.float32(-1000000000.0))
        row_max = jnp.max(scores, axis=-1, keepdims=True)
        weights = jnp.exp(scores - row_max)
        attn_probs = weights / jnp.sum(weights, axis=-1, keepdims=True)
        attn_probs = jnp.where(live_rows[None, :, None], attn_probs, jnp.float32(0.0))
        probs_b = attn_probs.astype(jnp.bfloat16)
        grad_v_list.append(
            jnp.einsum("hqk,qhd->kd", probs_b, o_group, preferred_element_type=jnp.float32)
        )
        dprob = jnp.einsum("qhd,kd->hqk", o_group, v_group, preferred_element_type=jnp.float32)
        row_delta = jnp.sum(attn_probs * dprob, axis=-1, keepdims=True)
        dscore = (attn_probs * (dprob - row_delta) * score_scale).astype(jnp.bfloat16)
        grad_q_list.append(
            jnp.einsum("hqk,kd->qhd", dscore, k_group, preferred_element_type=jnp.float32)
        )
        grad_k_list.append(
            jnp.einsum("hqk,qhd->kd", dscore, q_group, preferred_element_type=jnp.float32)
        )
    grad_q_rows = jnp.stack(grad_q_list, axis=1).reshape(row_count, HQ * DH).astype(jnp.bfloat16)
    grad_k_rows = jnp.stack(grad_k_list, axis=1).reshape(row_count, HK * DH).astype(jnp.bfloat16)
    grad_v_rows = jnp.stack(grad_v_list, axis=1).reshape(row_count, HK * DH).astype(jnp.bfloat16)
    return (grad_q_rows, grad_k_rows, grad_v_rows)


def local(hidden_in, queries, keys, values, grad_attn, send_rows, slot_docs):
    owners = lax.axis_size("dp")
    slot_count = send_rows.shape[0]
    tok_rows = queries.shape[0]
    live_send = send_rows >= 0
    pick_rows = jnp.maximum(send_rows, 0)
    grad_scale = 1.0 / math.sqrt(tok_rows * owners)

    def pack_rows(table):
        return jnp.where(live_send[:, :, None], table[pick_rows], jnp.zeros((), table.dtype))

    def flatten(block):
        return block.reshape(slot_count * owners, block.shape[2])

    def unflatten(block):
        return block.reshape(slot_count, owners, block.shape[1])

    targets = jnp.where(live_send, send_rows, tok_rows).reshape(-1)

    def place_rows(block):
        return (
            jnp.zeros((tok_rows, block.shape[2]), block.dtype)
            .at[targets]
            .set(flatten(block), mode="drop")
        )

    q_in, k_in, v_in, o_in = (
        lax.all_to_all(pack_rows(queries), "dp", split_axis=1, concat_axis=1, tiled=True),
        lax.all_to_all(pack_rows(keys), "dp", split_axis=1, concat_axis=1, tiled=True),
        lax.all_to_all(pack_rows(values), "dp", split_axis=1, concat_axis=1, tiled=True),
        lax.all_to_all(pack_rows(grad_attn), "dp", split_axis=1, concat_axis=1, tiled=True),
    )
    segment = jnp.broadcast_to(slot_docs[0][:, None], (slot_count, owners)).reshape(-1)
    grad_q_rows, grad_k_rows, grad_v_rows = attend_rows(
        flatten(q_in), flatten(k_in), flatten(v_in), flatten(o_in), segment
    )
    q_home, k_home, v_home = (
        lax.all_to_all(unflatten(grad_q_rows), "dp", split_axis=1, concat_axis=1, tiled=True),
        lax.all_to_all(unflatten(grad_k_rows), "dp", split_axis=1, concat_axis=1, tiled=True),
        lax.all_to_all(unflatten(grad_v_rows), "dp", split_axis=1, concat_axis=1, tiled=True),
    )
    grad_queries = place_rows(q_home)
    grad_keys = place_rows(k_home)
    grad_values = place_rows(v_home)
    partial = jnp.einsum("td,tc->dc", hidden_in, grad_values, preferred_element_type=jnp.float32)
    partial = partial.reshape(owners, partial.shape[0] // owners, partial.shape[1])
    grad_wv = lax.all_to_all(partial, "dp", 0, 0, tiled=True).sum(0) * grad_scale
    return (grad_queries, grad_keys, grad_values, grad_wv)


def solution(mesh):
    placed = (
        P("dp", None),
        P("dp", None),
        P("dp", None),
        P("dp", None),
        P("dp", None),
        P(),
        P("dp", None),
    )
    return jax.shard_map(
        local,
        mesh=mesh,
        in_specs=placed,
        out_specs=(P("dp", None), P("dp", None), P("dp", None), P("dp", None)),
        check_vma=False,
    )
```

```python
import math

import jax
import jax.numpy as jnp
from jax import lax
from jax.sharding import PartitionSpec as P

HQ = 16
HK = 4
DH = 128


def attend_rows(q_rows, k_rows, v_rows, o_rows, segment):
    row_count = q_rows.shape[0]
    group_size = HQ // HK
    score_scale = 1.0 / math.sqrt(DH)
    order_ids = jnp.arange(row_count, dtype=jnp.int32)
    live_rows = segment >= 0
    allowed = (
        (segment[:, None] == segment[None, :])
        & (order_ids[None, :] <= order_ids[:, None])
        & live_rows[:, None]
    )
    q_four = q_rows.reshape(row_count, HK, group_size, DH)
    o_four = o_rows.reshape(row_count, HK, group_size, DH)
    k_three = k_rows.reshape(row_count, HK, DH)
    v_three = v_rows.reshape(row_count, HK, DH)
    grad_q_list = []
    grad_k_list = []
    grad_v_list = []
    for head_kv in range(HK):
        q_group = q_four[:, head_kv]
        o_group = o_four[:, head_kv]
        k_group = k_three[:, head_kv]
        v_group = v_three[:, head_kv]
        scores = (
            jnp.einsum("qhd,kd->hqk", q_group, k_group, preferred_element_type=jnp.float32)
            * score_scale
        )
        scores = jnp.where(allowed[None], scores, jnp.float32(-1000000000.0))
        row_max = jnp.max(scores, axis=-1, keepdims=True)
        weights = jnp.exp(scores - row_max)
        attn_probs = weights / jnp.sum(weights, axis=-1, keepdims=True)
        attn_probs = jnp.where(live_rows[None, :, None], attn_probs, jnp.float32(0.0))
        probs_b = attn_probs.astype(jnp.bfloat16)
        grad_v_list.append(
            jnp.einsum("hqk,qhd->kd", probs_b, o_group, preferred_element_type=jnp.float32)
        )
        dprob = jnp.einsum("qhd,kd->hqk", o_group, v_group, preferred_element_type=jnp.float32)
        row_delta = jnp.sum(attn_probs * dprob, axis=-1, keepdims=True)
        dscore = (attn_probs * (dprob - row_delta) * score_scale).astype(jnp.bfloat16)
        grad_q_list.append(
            jnp.einsum("hqk,kd->qhd", dscore, k_group, preferred_element_type=jnp.float32)
        )
        grad_k_list.append(
            jnp.einsum("hqk,qhd->kd", dscore, q_group, preferred_element_type=jnp.float32)
        )
    grad_q_rows = jnp.stack(grad_q_list, axis=1).reshape(row_count, HQ * DH).astype(jnp.bfloat16)
    grad_k_rows = jnp.stack(grad_k_list, axis=1).reshape(row_count, HK * DH).astype(jnp.bfloat16)
    grad_v_rows = jnp.stack(grad_v_list, axis=1).reshape(row_count, HK * DH).astype(jnp.bfloat16)
    return (grad_q_rows, grad_k_rows, grad_v_rows)


def local(hidden_in, queries, keys, values, grad_attn, send_rows, slot_docs):
    owners = lax.axis_size("dp")
    slot_count = send_rows.shape[0]
    tok_rows = queries.shape[0]
    live_send = send_rows >= 0
    pick_rows = jnp.maximum(send_rows, 0)
    grad_scale = 1.0 / math.sqrt(tok_rows * owners)

    def pack_rows(table):
        return jnp.where(live_send[:, :, None], table[pick_rows], jnp.zeros((), table.dtype))

    def flatten(block):
        return block.reshape(slot_count * owners, block.shape[2])

    def unflatten(block):
        return block.reshape(slot_count, owners, block.shape[1])

    targets = jnp.where(live_send, send_rows, tok_rows).reshape(-1)

    def place_rows(block):
        return (
            jnp.zeros((tok_rows, block.shape[2]), block.dtype)
            .at[targets]
            .set(flatten(block), mode="drop")
        )

    widths = (queries.shape[1], keys.shape[1], values.shape[1], grad_attn.shape[1])
    bounds = [sum(widths[:i]) for i in range(len(widths) + 1)]
    table = jnp.concatenate((queries, keys, values, grad_attn), axis=1)
    rows_in = flatten(
        lax.all_to_all(pack_rows(table), "dp", split_axis=1, concat_axis=1, tiled=True)
    )
    q_in, k_in, v_in, o_in = (rows_in[:, bounds[i] : bounds[i + 1]] for i in range(len(widths)))
    segment = jnp.broadcast_to(slot_docs[0][:, None], (slot_count, owners)).reshape(-1)
    grad_q_rows, grad_k_rows, grad_v_rows = attend_rows(q_in, k_in, v_in, o_in, segment)
    rows_out = jnp.concatenate((grad_q_rows, grad_k_rows, grad_v_rows), axis=1)
    home = place_rows(
        lax.all_to_all(unflatten(rows_out), "dp", split_axis=1, concat_axis=1, tiled=True)
    )
    grad_queries = home[:, bounds[0] : bounds[1]]
    grad_keys = home[:, bounds[1] : bounds[2]]
    grad_values = home[:, bounds[2] : bounds[3]]
    partial = jnp.einsum("td,tc->dc", hidden_in, grad_values, preferred_element_type=jnp.float32)
    partial = partial.reshape(owners, partial.shape[0] // owners, partial.shape[1])
    grad_wv = lax.all_to_all(partial, "dp", 0, 0, tiled=True).sum(0) * grad_scale
    return (grad_queries, grad_keys, grad_values, grad_wv)


def solution(mesh):
    placed = (
        P("dp", None),
        P("dp", None),
        P("dp", None),
        P("dp", None),
        P("dp", None),
        P(),
        P("dp", None),
    )
    return jax.shard_map(
        local,
        mesh=mesh,
        in_specs=placed,
        out_specs=(P("dp", None), P("dp", None), P("dp", None), P("dp", None)),
        check_vma=False,
    )
```

```python
import math

import jax
import jax.numpy as jnp
from jax import lax
from jax.sharding import PartitionSpec as P

HQ = 16
HK = 4
DH = 128


def attend_group(q_group, k_group, v_group, o_group, segment):
    row_count = q_group.shape[0]
    group_size = HQ // HK
    score_scale = 1.0 / math.sqrt(DH)
    order_ids = jnp.arange(row_count, dtype=jnp.int32)
    live_rows = segment >= 0
    allowed = (
        (segment[:, None] == segment[None, :])
        & (order_ids[None, :] <= order_ids[:, None])
        & live_rows[:, None]
    )
    q_group = q_group.reshape(row_count, group_size, DH)
    o_group = o_group.reshape(row_count, group_size, DH)
    scores = (
        jnp.einsum("qhd,kd->hqk", q_group, k_group, preferred_element_type=jnp.float32)
        * score_scale
    )
    scores = jnp.where(allowed[None], scores, jnp.float32(-1000000000.0))
    row_max = jnp.max(scores, axis=-1, keepdims=True)
    weights = jnp.exp(scores - row_max)
    attn_probs = weights / jnp.sum(weights, axis=-1, keepdims=True)
    attn_probs = jnp.where(live_rows[None, :, None], attn_probs, jnp.float32(0.0))
    probs_b = attn_probs.astype(jnp.bfloat16)
    grad_v = jnp.einsum("hqk,qhd->kd", probs_b, o_group, preferred_element_type=jnp.float32)
    dprob = jnp.einsum("qhd,kd->hqk", o_group, v_group, preferred_element_type=jnp.float32)
    row_delta = jnp.sum(attn_probs * dprob, axis=-1, keepdims=True)
    dscore = (attn_probs * (dprob - row_delta) * score_scale).astype(jnp.bfloat16)
    grad_q = jnp.einsum("hqk,kd->qhd", dscore, k_group, preferred_element_type=jnp.float32)
    grad_k = jnp.einsum("hqk,qhd->kd", dscore, q_group, preferred_element_type=jnp.float32)
    return (
        grad_q.reshape(row_count, group_size * DH).astype(jnp.bfloat16),
        grad_k.astype(jnp.bfloat16),
        grad_v.astype(jnp.bfloat16),
    )


def local(hidden_in, queries, keys, values, grad_attn, send_rows, slot_docs):
    owners = lax.axis_size("dp")
    slot_count = send_rows.shape[0]
    tok_rows = queries.shape[0]
    live_send = send_rows >= 0
    pick_rows = jnp.maximum(send_rows, 0)
    grad_scale = 1.0 / math.sqrt(tok_rows * owners)

    def pack_rows(table):
        return jnp.where(live_send[:, :, None], table[pick_rows], jnp.zeros((), table.dtype))

    def flatten(block):
        return block.reshape(slot_count * owners, block.shape[2])

    def unflatten(block):
        return block.reshape(slot_count, owners, block.shape[1])

    targets = jnp.where(live_send, send_rows, tok_rows).reshape(-1)

    def place_rows(block):
        return (
            jnp.zeros((tok_rows, block.shape[2]), block.dtype)
            .at[targets]
            .set(flatten(block), mode="drop")
        )

    group_size = HQ // HK
    q_w, kv_w = group_size * DH, DH
    segment = jnp.broadcast_to(slot_docs[0][:, None], (slot_count, owners)).reshape(-1)
    dq_parts, dk_parts, dv_parts, wv_parts = [], [], [], []
    for head_kv in range(HK):
        q_cols = slice(head_kv * q_w, (head_kv + 1) * q_w)
        kv_cols = slice(head_kv * kv_w, (head_kv + 1) * kv_w)
        table = jnp.concatenate(
            (queries[:, q_cols], keys[:, kv_cols], values[:, kv_cols], grad_attn[:, q_cols]), axis=1
        )
        rows_in = flatten(
            lax.all_to_all(pack_rows(table), "dp", split_axis=1, concat_axis=1, tiled=True)
        )
        dq_rows, dk_rows, dv_rows = attend_group(
            rows_in[:, :q_w],
            rows_in[:, q_w : q_w + kv_w],
            rows_in[:, q_w + kv_w : q_w + 2 * kv_w],
            rows_in[:, q_w + 2 * kv_w :],
            segment,
        )
        rows_out = jnp.concatenate((dv_rows, dk_rows, dq_rows), axis=1)
        home = place_rows(
            lax.all_to_all(unflatten(rows_out), "dp", split_axis=1, concat_axis=1, tiled=True)
        )
        dv_home = home[:, :kv_w]
        dv_parts.append(dv_home)
        dk_parts.append(home[:, kv_w : 2 * kv_w])
        dq_parts.append(home[:, 2 * kv_w :])
        partial = jnp.einsum("td,tc->dc", hidden_in, dv_home, preferred_element_type=jnp.float32)
        partial = partial.reshape(owners, partial.shape[0] // owners, partial.shape[1])
        wv_parts.append(lax.all_to_all(partial, "dp", 0, 0, tiled=True).sum(0) * grad_scale)
    grad_queries = jnp.concatenate(dq_parts, axis=1)
    grad_keys = jnp.concatenate(dk_parts, axis=1)
    grad_values = jnp.concatenate(dv_parts, axis=1)
    grad_wv = jnp.concatenate(wv_parts, axis=1)
    return (grad_queries, grad_keys, grad_values, grad_wv)


def solution(mesh):
    placed = (
        P("dp", None),
        P("dp", None),
        P("dp", None),
        P("dp", None),
        P("dp", None),
        P(),
        P("dp", None),
    )
    return jax.shard_map(
        local,
        mesh=mesh,
        in_specs=placed,
        out_specs=(P("dp", None), P("dp", None), P("dp", None), P("dp", None)),
        check_vma=False,
    )
```

```python
import math

import jax
import jax.numpy as jnp
from jax import lax
from jax.sharding import Mesh, PartitionSpec as P
import numpy as np

HQ = 16
HK = 4
DH = 128


def attend_rows(q_rows, k_rows, v_rows, o_rows, segment):
    row_count = q_rows.shape[0]
    group_size = HQ // HK
    score_scale = 1.0 / math.sqrt(DH)
    order_ids = jnp.arange(row_count, dtype=jnp.int32)
    live_rows = segment >= 0
    allowed = (
        (segment[:, None] == segment[None, :])
        & (order_ids[None, :] <= order_ids[:, None])
        & live_rows[:, None]
    )
    q_four = q_rows.reshape(row_count, HK, group_size, DH)
    o_four = o_rows.reshape(row_count, HK, group_size, DH)
    k_three = k_rows.reshape(row_count, HK, DH)
    v_three = v_rows.reshape(row_count, HK, DH)
    grad_q_list = []
    grad_k_list = []
    grad_v_list = []
    for head_kv in range(HK):
        q_group = q_four[:, head_kv]
        o_group = o_four[:, head_kv]
        k_group = k_three[:, head_kv]
        v_group = v_three[:, head_kv]
        scores = (
            jnp.einsum("qhd,kd->hqk", q_group, k_group, preferred_element_type=jnp.float32)
            * score_scale
        )
        scores = jnp.where(allowed[None], scores, jnp.float32(-1000000000.0))
        row_max = jnp.max(scores, axis=-1, keepdims=True)
        weights = jnp.exp(scores - row_max)
        attn_probs = weights / jnp.sum(weights, axis=-1, keepdims=True)
        attn_probs = jnp.where(live_rows[None, :, None], attn_probs, jnp.float32(0.0))
        probs_b = attn_probs.astype(jnp.bfloat16)
        grad_v_list.append(
            jnp.einsum("hqk,qhd->kd", probs_b, o_group, preferred_element_type=jnp.float32)
        )
        dprob = jnp.einsum("qhd,kd->hqk", o_group, v_group, preferred_element_type=jnp.float32)
        row_delta = jnp.sum(attn_probs * dprob, axis=-1, keepdims=True)
        dscore = (attn_probs * (dprob - row_delta) * score_scale).astype(jnp.bfloat16)
        grad_q_list.append(
            jnp.einsum("hqk,kd->qhd", dscore, k_group, preferred_element_type=jnp.float32)
        )
        grad_k_list.append(
            jnp.einsum("hqk,qhd->kd", dscore, q_group, preferred_element_type=jnp.float32)
        )
    grad_q_rows = jnp.stack(grad_q_list, axis=1).reshape(row_count, HQ * DH).astype(jnp.bfloat16)
    grad_k_rows = jnp.stack(grad_k_list, axis=1).reshape(row_count, HK * DH).astype(jnp.bfloat16)
    grad_v_rows = jnp.stack(grad_v_list, axis=1).reshape(row_count, HK * DH).astype(jnp.bfloat16)
    return (grad_q_rows, grad_k_rows, grad_v_rows)


CHIP, CORE = "chip", "core"
DP = (CHIP, CORE)


def local(hidden_in, queries, keys, values, grad_attn, send_rows, slot_docs):
    chips, cores = lax.axis_size(CHIP), lax.axis_size(CORE)
    owners = chips * cores
    slot_count = send_rows.shape[0]
    tok_rows = queries.shape[0]
    live_send = send_rows >= 0
    pick_rows = jnp.maximum(send_rows, 0)
    grad_scale = 1.0 / math.sqrt(tok_rows * owners)

    def pack_rows(table):
        return jnp.where(live_send[:, :, None], table[pick_rows], jnp.zeros((), table.dtype))

    def flatten(block):
        return block.reshape(slot_count * owners, block.shape[2])

    def unflatten(block):
        return block.reshape(slot_count, owners, block.shape[1])

    targets = jnp.where(live_send, send_rows, tok_rows).reshape(-1)

    def place_rows(block):
        return (
            jnp.zeros((tok_rows, block.shape[2]), block.dtype)
            .at[targets]
            .set(flatten(block), mode="drop")
        )

    q_in, k_in, v_in, o_in = (
        lax.all_to_all(pack_rows(queries), DP, split_axis=1, concat_axis=1, tiled=True),
        lax.all_to_all(pack_rows(keys), DP, split_axis=1, concat_axis=1, tiled=True),
        lax.all_to_all(pack_rows(values), DP, split_axis=1, concat_axis=1, tiled=True),
        lax.all_to_all(pack_rows(grad_attn), DP, split_axis=1, concat_axis=1, tiled=True),
    )
    segment = jnp.broadcast_to(slot_docs[0][:, None], (slot_count, owners)).reshape(-1)
    grad_q_rows, grad_k_rows, grad_v_rows = attend_rows(
        flatten(q_in), flatten(k_in), flatten(v_in), flatten(o_in), segment
    )
    q_home, k_home, v_home = (
        lax.all_to_all(unflatten(grad_q_rows), DP, split_axis=1, concat_axis=1, tiled=True),
        lax.all_to_all(unflatten(grad_k_rows), DP, split_axis=1, concat_axis=1, tiled=True),
        lax.all_to_all(unflatten(grad_v_rows), DP, split_axis=1, concat_axis=1, tiled=True),
    )
    grad_queries = place_rows(q_home)
    grad_keys = place_rows(k_home)
    grad_values = place_rows(v_home)
    core = lax.axis_index(CORE)
    swap = [(0, 1), (1, 0)]
    blocks = hidden_in.reshape(tok_rows, chips, cores, -1)
    mine = lax.dynamic_index_in_dim(blocks, core, axis=2, keepdims=False)
    theirs = lax.dynamic_index_in_dim(blocks, 1 - core, axis=2, keepdims=False)
    from_partner = lax.ppermute(theirs, CORE, swap)
    hidden_pair = jnp.concatenate((mine, from_partner), axis=0).reshape(2 * tok_rows, -1)
    grad_pair = jnp.concatenate((grad_values, lax.ppermute(grad_values, CORE, swap)), axis=0)
    partial = jnp.einsum("td,tc->dc", hidden_pair, grad_pair, preferred_element_type=jnp.float32)
    partial = partial.reshape(chips, partial.shape[0] // chips, partial.shape[1])
    grad_wv = lax.all_to_all(partial, CHIP, 0, 0, tiled=True).sum(0) * grad_scale
    return (grad_queries, grad_keys, grad_values, grad_wv)


def solution(mesh):
    devices = np.asarray(mesh.devices).reshape(-1)
    pair_mesh = Mesh(devices.reshape(-1, 2), DP)
    rows = P(DP, None)
    placed = (rows, rows, rows, rows, rows, P(), rows)
    return jax.shard_map(
        local,
        mesh=pair_mesh,
        in_specs=placed,
        out_specs=(rows, rows, rows, rows),
        check_vma=False,
    )
```

```python
import math

import jax
import jax.numpy as jnp
from jax import lax
from jax.sharding import Mesh, PartitionSpec as P
import numpy as np
from jax.experimental import pallas as pl
from jax.experimental.pallas import tpu as pltpu

HQ = 16
HK = 4
DH = 128
INTERPRET = False


NT = (((1,), (1,)), ((), ()))
TN = (((0,), (0,)), ((), ()))


def attend_kernel(seg_col_ref, seg_row_ref, q_ref, k_ref, v_ref, o_ref, dq_ref, dk_ref, dv_ref):
    row_count = q_ref.shape[0]
    group_size = HQ // HK
    score_scale = 1.0 / math.sqrt(DH)
    seg_col = seg_col_ref[...]
    live_rows = seg_col >= 0
    row_ids = lax.broadcasted_iota(jnp.int32, (row_count, row_count), 0)
    col_ids = lax.broadcasted_iota(jnp.int32, (row_count, row_count), 1)
    allowed = (seg_col == seg_row_ref[...]) & (col_ids <= row_ids) & live_rows
    k_group = k_ref[...]
    v_group = v_ref[...]
    dk_acc = jnp.zeros((row_count, DH), jnp.float32)
    dv_acc = jnp.zeros((row_count, DH), jnp.float32)
    for head in range(group_size):
        cols = slice(head * DH, (head + 1) * DH)
        q_head = q_ref[:, cols]
        o_head = o_ref[:, cols]
        scores = lax.dot_general(q_head, k_group, NT, preferred_element_type=jnp.float32)
        scores = jnp.where(allowed, scores * score_scale, jnp.float32(-1000000000.0))
        row_max = jnp.max(scores, axis=1, keepdims=True)
        weights = jnp.exp(scores - row_max)
        attn_probs = weights / jnp.sum(weights, axis=1, keepdims=True)
        attn_probs = jnp.where(live_rows, attn_probs, jnp.float32(0.0))
        probs_b = attn_probs.astype(jnp.bfloat16)
        dv_acc = dv_acc + lax.dot_general(probs_b, o_head, TN, preferred_element_type=jnp.float32)
        dprob = lax.dot_general(o_head, v_group, NT, preferred_element_type=jnp.float32)
        row_delta = jnp.sum(attn_probs * dprob, axis=1, keepdims=True)
        dscore = (attn_probs * (dprob - row_delta) * score_scale).astype(jnp.bfloat16)
        dq_ref[:, cols] = jnp.dot(dscore, k_group, preferred_element_type=jnp.float32).astype(
            dq_ref.dtype
        )
        dk_acc = dk_acc + lax.dot_general(dscore, q_head, TN, preferred_element_type=jnp.float32)
    dk_ref[...] = dk_acc.astype(dk_ref.dtype)
    dv_ref[...] = dv_acc.astype(dv_ref.dtype)


def attend_rows(q_rows, k_rows, v_rows, o_rows, segment):
    row_count = q_rows.shape[0]
    q_w = (HQ // HK) * DH
    seg = segment.astype(jnp.int32)
    whole = lambda g: (0, 0)
    q_spec = pl.BlockSpec((row_count, q_w), lambda g: (0, g))
    kv_spec = pl.BlockSpec((row_count, DH), lambda g: (0, g))
    return pl.pallas_call(
        attend_kernel,
        grid=(HK,),
        in_specs=[
            pl.BlockSpec((row_count, 1), whole),
            pl.BlockSpec((1, row_count), whole),
            q_spec,
            kv_spec,
            kv_spec,
            q_spec,
        ],
        out_specs=[q_spec, kv_spec, kv_spec],
        out_shape=[
            jax.ShapeDtypeStruct(q_rows.shape, jnp.bfloat16),
            jax.ShapeDtypeStruct(k_rows.shape, jnp.bfloat16),
            jax.ShapeDtypeStruct(v_rows.shape, jnp.bfloat16),
        ],
        compiler_params=pltpu.CompilerParams(dimension_semantics=("arbitrary",)),
        interpret=INTERPRET,
    )(seg.reshape(row_count, 1), seg.reshape(1, row_count), q_rows, k_rows, v_rows, o_rows)


CHIP, CORE = "chip", "core"
DP = (CHIP, CORE)


def local(hidden_in, queries, keys, values, grad_attn, send_rows, slot_docs):
    chips, cores = lax.axis_size(CHIP), lax.axis_size(CORE)
    owners = chips * cores
    slot_count = send_rows.shape[0]
    tok_rows = queries.shape[0]
    live_send = send_rows >= 0
    pick_rows = jnp.maximum(send_rows, 0)
    grad_scale = 1.0 / math.sqrt(tok_rows * owners)

    def pack_rows(table):
        return jnp.where(live_send[:, :, None], table[pick_rows], jnp.zeros((), table.dtype))

    def flatten(block):
        return block.reshape(slot_count * owners, block.shape[2])

    def unflatten(block):
        return block.reshape(slot_count, owners, block.shape[1])

    targets = jnp.where(live_send, send_rows, tok_rows).reshape(-1)

    def place_rows(block):
        return (
            jnp.zeros((tok_rows, block.shape[2]), block.dtype)
            .at[targets]
            .set(flatten(block), mode="drop")
        )

    q_in, k_in, v_in, o_in = (
        lax.all_to_all(pack_rows(queries), DP, split_axis=1, concat_axis=1, tiled=True),
        lax.all_to_all(pack_rows(keys), DP, split_axis=1, concat_axis=1, tiled=True),
        lax.all_to_all(pack_rows(values), DP, split_axis=1, concat_axis=1, tiled=True),
        lax.all_to_all(pack_rows(grad_attn), DP, split_axis=1, concat_axis=1, tiled=True),
    )
    segment = jnp.broadcast_to(slot_docs[0][:, None], (slot_count, owners)).reshape(-1)
    grad_q_rows, grad_k_rows, grad_v_rows = attend_rows(
        flatten(q_in), flatten(k_in), flatten(v_in), flatten(o_in), segment
    )
    q_home, k_home, v_home = (
        lax.all_to_all(unflatten(grad_q_rows), DP, split_axis=1, concat_axis=1, tiled=True),
        lax.all_to_all(unflatten(grad_k_rows), DP, split_axis=1, concat_axis=1, tiled=True),
        lax.all_to_all(unflatten(grad_v_rows), DP, split_axis=1, concat_axis=1, tiled=True),
    )
    grad_queries = place_rows(q_home)
    grad_keys = place_rows(k_home)
    grad_values = place_rows(v_home)
    core = lax.axis_index(CORE)
    swap = [(0, 1), (1, 0)]
    blocks = hidden_in.reshape(tok_rows, chips, cores, -1)
    mine = lax.dynamic_index_in_dim(blocks, core, axis=2, keepdims=False)
    theirs = lax.dynamic_index_in_dim(blocks, 1 - core, axis=2, keepdims=False)
    from_partner = lax.ppermute(theirs, CORE, swap)
    hidden_pair = jnp.concatenate((mine, from_partner), axis=0).reshape(2 * tok_rows, -1)
    grad_pair = jnp.concatenate((grad_values, lax.ppermute(grad_values, CORE, swap)), axis=0)
    partial = jnp.einsum("td,tc->dc", hidden_pair, grad_pair, preferred_element_type=jnp.float32)
    partial = partial.reshape(chips, partial.shape[0] // chips, partial.shape[1])
    grad_wv = lax.all_to_all(partial, CHIP, 0, 0, tiled=True).sum(0) * grad_scale
    return (grad_queries, grad_keys, grad_values, grad_wv)


def solution(mesh):
    devices = np.asarray(mesh.devices).reshape(-1)
    pair_mesh = Mesh(devices.reshape(-1, 2), DP)
    rows = P(DP, None)
    placed = (rows, rows, rows, rows, rows, P(), rows)
    return jax.shard_map(
        local,
        mesh=pair_mesh,
        in_specs=placed,
        out_specs=(rows, rows, rows, rows),
        check_vma=False,
    )
```

```python
import math

import jax
import jax.numpy as jnp
from jax import lax
from jax.sharding import Mesh, PartitionSpec as P
import numpy as np
from jax.experimental import pallas as pl
from jax.experimental.pallas import tpu as pltpu

HQ = 16
HK = 4
DH = 128
INTERPRET = False


NT = (((1,), (1,)), ((), ()))
TN = (((0,), (0,)), ((), ()))


def attend_kernel(seg_col_ref, seg_row_ref, key_col_ref, key_row_ref, rows_ref, out_ref):
    row_count = rows_ref.shape[0]
    group_size = HQ // HK
    q_w = group_size * DH
    score_scale = 1.0 / math.sqrt(DH)
    seg_col = seg_col_ref[...]
    live_rows = seg_col >= 0
    allowed = (
        (seg_col == seg_row_ref[...]) & (key_row_ref[...] <= key_col_ref[...]) & live_rows
    )
    k_group = rows_ref[:, q_w : q_w + DH]
    v_group = rows_ref[:, q_w + DH : q_w + 2 * DH]
    o_base = q_w + 2 * DH
    dk_acc = jnp.zeros((row_count, DH), jnp.float32)
    dv_acc = jnp.zeros((row_count, DH), jnp.float32)
    for head in range(group_size):
        q_head = rows_ref[:, head * DH : (head + 1) * DH]
        o_head = rows_ref[:, o_base + head * DH : o_base + (head + 1) * DH]
        scores = lax.dot_general(q_head, k_group, NT, preferred_element_type=jnp.float32)
        scores = jnp.where(allowed, scores * score_scale, jnp.float32(-1000000000.0))
        row_max = jnp.max(scores, axis=1, keepdims=True)
        weights = jnp.exp(scores - row_max)
        attn_probs = weights / jnp.sum(weights, axis=1, keepdims=True)
        attn_probs = jnp.where(live_rows, attn_probs, jnp.float32(0.0))
        probs_b = attn_probs.astype(jnp.bfloat16)
        dv_acc = dv_acc + lax.dot_general(probs_b, o_head, TN, preferred_element_type=jnp.float32)
        dprob = lax.dot_general(o_head, v_group, NT, preferred_element_type=jnp.float32)
        row_delta = jnp.sum(attn_probs * dprob, axis=1, keepdims=True)
        dscore = (attn_probs * (dprob - row_delta) * score_scale).astype(jnp.bfloat16)
        out_ref[:, head * DH : (head + 1) * DH] = jnp.dot(
            dscore, k_group, preferred_element_type=jnp.float32
        ).astype(out_ref.dtype)
        dk_acc = dk_acc + lax.dot_general(dscore, q_head, TN, preferred_element_type=jnp.float32)
    out_ref[:, q_w : q_w + DH] = dk_acc.astype(out_ref.dtype)
    out_ref[:, q_w + DH : q_w + 2 * DH] = dv_acc.astype(out_ref.dtype)


def attend_rows(rows_in, segment, order_key):
    row_count = rows_in.shape[0]
    q_w = (HQ // HK) * DH
    in_w, out_w = 2 * q_w + 2 * DH, q_w + 2 * DH
    whole = lambda g: (0, 0)
    col = pl.BlockSpec((row_count, 1), whole)
    row = pl.BlockSpec((1, row_count), whole)
    return pl.pallas_call(
        attend_kernel,
        grid=(HK,),
        in_specs=[col, row, col, row, pl.BlockSpec((row_count, in_w), lambda g: (0, g))],
        out_specs=pl.BlockSpec((row_count, out_w), lambda g: (0, g)),
        out_shape=jax.ShapeDtypeStruct((row_count, HK * out_w), jnp.bfloat16),
        compiler_params=pltpu.CompilerParams(dimension_semantics=("arbitrary",)),
        interpret=INTERPRET,
    )(
        segment.reshape(row_count, 1),
        segment.reshape(1, row_count),
        order_key.reshape(row_count, 1),
        order_key.reshape(1, row_count),
        rows_in,
    )


CHIP, CORE = "chip", "core"
DP = (CHIP, CORE)


def local(hidden_in, queries, keys, values, grad_attn, send_rows, slot_docs):
    chips, cores = lax.axis_size(CHIP), lax.axis_size(CORE)
    owners = chips * cores
    slot_count = send_rows.shape[0]
    tok_rows = queries.shape[0]
    group_size = HQ // HK
    q_w = group_size * DH
    live_send = (send_rows >= 0).T
    pick_rows = jnp.maximum(send_rows, 0).T
    grad_scale = 1.0 / math.sqrt(tok_rows * owners)
    pieces = []
    for head_kv in range(HK):
        pieces += [
            queries[:, head_kv * q_w : (head_kv + 1) * q_w],
            keys[:, head_kv * DH : (head_kv + 1) * DH],
            values[:, head_kv * DH : (head_kv + 1) * DH],
            grad_attn[:, head_kv * q_w : (head_kv + 1) * q_w],
        ]
    table = jnp.concatenate(pieces, axis=1)
    rows_in = lax.all_to_all(table[pick_rows], DP, 0, 0, tiled=True)
    rows_in = rows_in.reshape(owners * slot_count, table.shape[1])
    row_ids = jnp.arange(owners * slot_count, dtype=jnp.int32)
    order_key = (row_ids % slot_count) * owners + row_ids // slot_count
    segment = jnp.tile(slot_docs[0].astype(jnp.int32), owners)
    rows_out = attend_rows(rows_in, segment, order_key)
    back = lax.all_to_all(
        rows_out.reshape(owners, slot_count, rows_out.shape[1]), DP, 0, 0, tiled=True
    )
    targets = jnp.where(live_send, pick_rows, tok_rows).reshape(-1)
    home = (
        jnp.zeros((tok_rows, back.shape[2]), back.dtype)
        .at[targets]
        .set(back.reshape(owners * slot_count, back.shape[2]), mode="drop")
    )
    out_w = q_w + 2 * DH
    grad_queries = jnp.concatenate(
        [home[:, g * out_w : g * out_w + q_w] for g in range(HK)], axis=1
    )
    grad_keys = jnp.concatenate(
        [home[:, g * out_w + q_w : g * out_w + q_w + DH] for g in range(HK)], axis=1
    )
    grad_values = jnp.concatenate(
        [home[:, g * out_w + q_w + DH : (g + 1) * out_w] for g in range(HK)], axis=1
    )
    core = lax.axis_index(CORE)
    swap = [(0, 1), (1, 0)]
    blocks = hidden_in.reshape(tok_rows, chips, cores, -1)
    mine = lax.dynamic_index_in_dim(blocks, core, axis=2, keepdims=False)
    theirs = lax.dynamic_index_in_dim(blocks, 1 - core, axis=2, keepdims=False)
    from_partner = lax.ppermute(theirs, CORE, swap)
    hidden_pair = jnp.concatenate((mine, from_partner), axis=0).reshape(2 * tok_rows, -1)
    grad_pair = jnp.concatenate((grad_values, lax.ppermute(grad_values, CORE, swap)), axis=0)
    partial = jnp.einsum("td,tc->dc", hidden_pair, grad_pair, preferred_element_type=jnp.float32)
    partial = partial.reshape(chips, partial.shape[0] // chips, partial.shape[1])
    grad_wv = lax.all_to_all(partial, CHIP, 0, 0, tiled=True).sum(0) * grad_scale
    return (grad_queries, grad_keys, grad_values, grad_wv)


def solution(mesh):
    devices = np.asarray(mesh.devices).reshape(-1)
    pair_mesh = Mesh(devices.reshape(-1, 2), DP)
    rows = P(DP, None)
    placed = (rows, rows, rows, rows, rows, P(), rows)
    return jax.shard_map(
        local,
        mesh=pair_mesh,
        in_specs=placed,
        out_specs=(rows, rows, rows, rows),
        check_vma=False,
    )
```

```python
import math

import jax
import jax.numpy as jnp
from jax import lax
from jax.sharding import Mesh, PartitionSpec as P
import numpy as np
from jax.experimental import pallas as pl
from jax.experimental.pallas import tpu as pltpu

HQ = 16
HK = 4
DH = 128
INTERPRET = False


NT = (((1,), (1,)), ((), ()))
TN = (((0,), (0,)), ((), ()))


def attend_kernel(
    seg_col_ref, seg_row_ref, key_col_ref, key_row_ref, q_ref, k_ref, v_ref, o_ref, out_ref
):
    row_count = q_ref.shape[0]
    group_size = HQ // HK
    q_w = group_size * DH
    score_scale = 1.0 / math.sqrt(DH)
    seg_col = seg_col_ref[...]
    live_rows = seg_col >= 0
    allowed = (
        (seg_col == seg_row_ref[...]) & (key_row_ref[...] <= key_col_ref[...]) & live_rows
    )
    k_group = k_ref[...]
    v_group = v_ref[...]
    dk_acc = jnp.zeros((row_count, DH), jnp.float32)
    dv_acc = jnp.zeros((row_count, DH), jnp.float32)
    for head in range(group_size):
        q_head = q_ref[:, head * DH : (head + 1) * DH]
        o_head = o_ref[:, head * DH : (head + 1) * DH]
        scores = lax.dot_general(q_head, k_group, NT, preferred_element_type=jnp.float32)
        scores = jnp.where(allowed, scores * score_scale, jnp.float32(-1000000000.0))
        row_max = jnp.max(scores, axis=1, keepdims=True)
        weights = jnp.exp(scores - row_max)
        attn_probs = weights * (1.0 / jnp.sum(weights, axis=1, keepdims=True))
        attn_probs = jnp.where(live_rows, attn_probs, jnp.float32(0.0))
        probs_b = attn_probs.astype(jnp.bfloat16)
        dv_acc = dv_acc + lax.dot_general(probs_b, o_head, TN, preferred_element_type=jnp.float32)
        dprob = lax.dot_general(o_head, v_group, NT, preferred_element_type=jnp.float32)
        row_delta = jnp.sum(attn_probs * dprob, axis=1, keepdims=True)
        dscore = (attn_probs * (dprob - row_delta) * score_scale).astype(jnp.bfloat16)
        out_ref[:, head * DH : (head + 1) * DH] = jnp.dot(
            dscore, k_group, preferred_element_type=jnp.float32
        ).astype(out_ref.dtype)
        dk_acc = dk_acc + lax.dot_general(dscore, q_head, TN, preferred_element_type=jnp.float32)
    out_ref[:, q_w : q_w + DH] = dk_acc.astype(out_ref.dtype)
    out_ref[:, q_w + DH : q_w + 2 * DH] = dv_acc.astype(out_ref.dtype)


def attend_rows(rows_in, segment, order_key):
    row_count = rows_in.shape[0]
    q_w = (HQ // HK) * DH
    out_w = q_w + 2 * DH
    k_at, v_at, o_at = HK * q_w // DH, HK * q_w // DH + HK, (HK * q_w + 2 * HK * DH) // q_w
    whole = lambda g: (0, 0)
    col = pl.BlockSpec((row_count, 1), whole)
    row = pl.BlockSpec((1, row_count), whole)
    return pl.pallas_call(
        attend_kernel,
        grid=(HK,),
        in_specs=[
            col,
            row,
            col,
            row,
            pl.BlockSpec((row_count, q_w), lambda g: (0, g)),
            pl.BlockSpec((row_count, DH), lambda g: (0, k_at + g)),
            pl.BlockSpec((row_count, DH), lambda g: (0, v_at + g)),
            pl.BlockSpec((row_count, q_w), lambda g: (0, o_at + g)),
        ],
        out_specs=pl.BlockSpec((row_count, out_w), lambda g: (0, g)),
        out_shape=jax.ShapeDtypeStruct((row_count, HK * out_w), jnp.bfloat16),
        compiler_params=pltpu.CompilerParams(dimension_semantics=("arbitrary",)),
        interpret=INTERPRET,
    )(
        segment.reshape(row_count, 1),
        segment.reshape(1, row_count),
        order_key.reshape(row_count, 1),
        order_key.reshape(1, row_count),
        rows_in,
        rows_in,
        rows_in,
        rows_in,
    )


CHIP, CORE = "chip", "core"
DP = (CHIP, CORE)


def local(hidden_in, queries, keys, values, grad_attn, send_rows, slot_docs):
    chips, cores = lax.axis_size(CHIP), lax.axis_size(CORE)
    owners = chips * cores
    slot_count = send_rows.shape[0]
    tok_rows = queries.shape[0]
    group_size = HQ // HK
    q_w = group_size * DH
    live_send = (send_rows >= 0).T
    pick_rows = jnp.maximum(send_rows, 0).T
    grad_scale = 1.0 / math.sqrt(tok_rows * owners)
    table = jnp.concatenate((queries, keys, values, grad_attn), axis=1)
    rows_in = lax.all_to_all(table[pick_rows], DP, 0, 0, tiled=True)
    rows_in = rows_in.reshape(owners * slot_count, table.shape[1])
    row_ids = jnp.arange(owners * slot_count, dtype=jnp.int32)
    order_key = (row_ids % slot_count) * owners + row_ids // slot_count
    segment = jnp.tile(slot_docs[0].astype(jnp.int32), owners)
    rows_out = attend_rows(rows_in, segment, order_key)
    back = lax.all_to_all(
        rows_out.reshape(owners, slot_count, rows_out.shape[1]), DP, 0, 0, tiled=True
    )
    targets = jnp.where(live_send, pick_rows, tok_rows).reshape(-1)
    home = (
        jnp.zeros((tok_rows, back.shape[2]), back.dtype)
        .at[targets]
        .set(back.reshape(owners * slot_count, back.shape[2]), mode="drop")
    )
    out_w = q_w + 2 * DH
    grad_queries = jnp.concatenate(
        [home[:, g * out_w : g * out_w + q_w] for g in range(HK)], axis=1
    )
    grad_keys = jnp.concatenate(
        [home[:, g * out_w + q_w : g * out_w + q_w + DH] for g in range(HK)], axis=1
    )
    grad_values = jnp.concatenate(
        [home[:, g * out_w + q_w + DH : (g + 1) * out_w] for g in range(HK)], axis=1
    )
    core = lax.axis_index(CORE)
    swap = [(0, 1), (1, 0)]
    blocks = hidden_in.reshape(tok_rows, chips, cores, -1)
    mine = lax.dynamic_index_in_dim(blocks, core, axis=2, keepdims=False)
    theirs = lax.dynamic_index_in_dim(blocks, 1 - core, axis=2, keepdims=False)
    from_partner = lax.ppermute(theirs, CORE, swap)
    hidden_pair = jnp.concatenate((mine, from_partner), axis=0).reshape(2 * tok_rows, -1)
    grad_pair = jnp.concatenate((grad_values, lax.ppermute(grad_values, CORE, swap)), axis=0)
    partial = jnp.einsum("td,tc->dc", hidden_pair, grad_pair, preferred_element_type=jnp.float32)
    partial = partial.reshape(chips, partial.shape[0] // chips, partial.shape[1])
    grad_wv = lax.all_to_all(partial, CHIP, 0, 0, tiled=True).sum(0) * grad_scale
    return (grad_queries, grad_keys, grad_values, grad_wv)


def solution(mesh):
    devices = np.asarray(mesh.devices).reshape(-1)
    pair_mesh = Mesh(devices.reshape(-1, 2), DP)
    rows = P(DP, None)
    placed = (rows, rows, rows, rows, rows, P(), rows)
    return jax.shard_map(
        local,
        mesh=pair_mesh,
        in_specs=placed,
        out_specs=(rows, rows, rows, rows),
        check_vma=False,
    )
```

```python
import math

import jax
import jax.numpy as jnp
from jax import lax
from jax.sharding import Mesh, PartitionSpec as P
import numpy as np
from jax.experimental import pallas as pl
from jax.experimental.pallas import tpu as pltpu

HQ = 16
HK = 4
DH = 128
INTERPRET = False


NT = (((1,), (1,)), ((), ()))
TN = (((0,), (0,)), ((), ()))


def attend_kernel(
    seg_col_ref, seg_row_ref, key_col_ref, key_row_ref, q_ref, k_ref, v_ref, o_ref, out_ref
):
    row_count = q_ref.shape[0]
    group_size = HQ // HK
    q_w = group_size * DH
    score_scale = 1.0 / math.sqrt(DH)
    seg_col = seg_col_ref[...]
    live_rows = seg_col >= 0
    allowed = (
        (seg_col == seg_row_ref[...]) & (key_row_ref[...] <= key_col_ref[...]) & live_rows
    )
    k_group = k_ref[...]
    v_group = v_ref[...]
    dk_acc = jnp.zeros((row_count, DH), jnp.float32)
    dv_acc = jnp.zeros((row_count, DH), jnp.float32)
    for head in range(group_size):
        q_head = q_ref[:, head * DH : (head + 1) * DH]
        o_head = o_ref[:, head * DH : (head + 1) * DH]
        scores = lax.dot_general(q_head, k_group, NT, preferred_element_type=jnp.float32)
        scores = jnp.where(allowed, scores * score_scale, jnp.float32(-1000000000.0))
        row_max = jnp.max(scores, axis=1, keepdims=True)
        weights = jnp.exp(scores - row_max)
        attn_probs = weights * (1.0 / jnp.sum(weights, axis=1, keepdims=True))
        attn_probs = jnp.where(live_rows, attn_probs, jnp.float32(0.0))
        probs_b = attn_probs.astype(jnp.bfloat16)
        dv_acc = dv_acc + lax.dot_general(probs_b, o_head, TN, preferred_element_type=jnp.float32)
        dprob = lax.dot_general(o_head, v_group, NT, preferred_element_type=jnp.float32)
        row_delta = jnp.sum(attn_probs * dprob, axis=1, keepdims=True)
        dscore = (attn_probs * (dprob - row_delta) * score_scale).astype(jnp.bfloat16)
        out_ref[:, head * DH : (head + 1) * DH] = jnp.dot(
            dscore, k_group, preferred_element_type=jnp.float32
        ).astype(out_ref.dtype)
        dk_acc = dk_acc + lax.dot_general(dscore, q_head, TN, preferred_element_type=jnp.float32)
    out_ref[:, q_w : q_w + DH] = dk_acc.astype(out_ref.dtype)
    out_ref[:, q_w + DH : q_w + 2 * DH] = dv_acc.astype(out_ref.dtype)


def attend_rows(rows_in, segment, order_key):
    row_count = rows_in.shape[0]
    q_w = (HQ // HK) * DH
    out_w = q_w + 2 * DH
    k_at, v_at, o_at = HK * q_w // DH, HK * q_w // DH + HK, (HK * q_w + 2 * HK * DH) // q_w
    whole = lambda g: (0, 0)
    col = pl.BlockSpec((row_count, 1), whole)
    row = pl.BlockSpec((1, row_count), whole)
    return pl.pallas_call(
        attend_kernel,
        grid=(HK,),
        in_specs=[
            col,
            row,
            col,
            row,
            pl.BlockSpec((row_count, q_w), lambda g: (0, g)),
            pl.BlockSpec((row_count, DH), lambda g: (0, k_at + g)),
            pl.BlockSpec((row_count, DH), lambda g: (0, v_at + g)),
            pl.BlockSpec((row_count, q_w), lambda g: (0, o_at + g)),
        ],
        out_specs=pl.BlockSpec((row_count, out_w), lambda g: (0, g)),
        out_shape=jax.ShapeDtypeStruct((row_count, HK * out_w), jnp.bfloat16),
        compiler_params=pltpu.CompilerParams(dimension_semantics=("arbitrary",)),
        interpret=INTERPRET,
    )(
        segment.reshape(row_count, 1),
        segment.reshape(1, row_count),
        order_key.reshape(row_count, 1),
        order_key.reshape(1, row_count),
        rows_in,
        rows_in,
        rows_in,
        rows_in,
    )


OUTER, INNER = "outer", "inner"
DP = (OUTER, INNER)
GROUP = 8


def local(hidden_in, queries, keys, values, grad_attn, send_rows, slot_docs):
    outers, groups = lax.axis_size(OUTER), lax.axis_size(INNER)
    owners = outers * groups
    slot_count = send_rows.shape[0]
    tok_rows = queries.shape[0]
    group_size = HQ // HK
    q_w = group_size * DH
    live_send = (send_rows >= 0).T
    pick_rows = jnp.maximum(send_rows, 0).T
    grad_scale = 1.0 / math.sqrt(tok_rows * owners)
    table = jnp.concatenate((queries, keys, values, grad_attn), axis=1)
    rows_in = lax.all_to_all(table[pick_rows], DP, 0, 0, tiled=True)
    rows_in = rows_in.reshape(owners * slot_count, table.shape[1])
    row_ids = jnp.arange(owners * slot_count, dtype=jnp.int32)
    order_key = (row_ids % slot_count) * owners + row_ids // slot_count
    segment = jnp.tile(slot_docs[0].astype(jnp.int32), owners)
    rows_out = attend_rows(rows_in, segment, order_key)
    back = lax.all_to_all(
        rows_out.reshape(owners, slot_count, rows_out.shape[1]), DP, 0, 0, tiled=True
    )
    targets = jnp.where(live_send, pick_rows, tok_rows).reshape(-1)
    home = (
        jnp.zeros((tok_rows, back.shape[2]), back.dtype)
        .at[targets]
        .set(back.reshape(owners * slot_count, back.shape[2]), mode="drop")
    )
    out_w = q_w + 2 * DH
    grad_queries = jnp.concatenate(
        [home[:, g * out_w : g * out_w + q_w] for g in range(HK)], axis=1
    )
    grad_keys = jnp.concatenate(
        [home[:, g * out_w + q_w : g * out_w + q_w + DH] for g in range(HK)], axis=1
    )
    grad_values = jnp.concatenate(
        [home[:, g * out_w + q_w + DH : (g + 1) * out_w] for g in range(HK)], axis=1
    )
    me = lax.axis_index(INNER)
    shifts = range(1, groups)
    blocks = hidden_in.reshape(tok_rows, outers, groups, -1)
    hidden_grp = [lax.dynamic_index_in_dim(blocks, me, axis=2, keepdims=False)]
    for shift in shifts:
        ring = [(i, (i + shift) % groups) for i in range(groups)]
        theirs = lax.dynamic_index_in_dim(blocks, (me + shift) % groups, axis=2, keepdims=False)
        hidden_grp.append(lax.ppermute(theirs, INNER, ring))
    grad_grp = [grad_values]
    for shift in shifts:
        ring = [(i, (i + shift) % groups) for i in range(groups)]
        grad_grp.append(lax.ppermute(grad_values, INNER, ring))
    hidden_grp = jnp.concatenate(hidden_grp, axis=0).reshape(groups * tok_rows, -1)
    grad_grp = jnp.concatenate(grad_grp, axis=0)
    partial = jnp.einsum("td,tc->dc", hidden_grp, grad_grp, preferred_element_type=jnp.float32)
    partial = partial.reshape(outers, partial.shape[0] // outers, partial.shape[1])
    grad_wv = lax.all_to_all(partial, OUTER, 0, 0, tiled=True).sum(0) * grad_scale
    return (grad_queries, grad_keys, grad_values, grad_wv)


def solution(mesh):
    devices = np.asarray(mesh.devices).reshape(-1)
    group = GROUP if devices.size % GROUP == 0 else 1
    pair_mesh = Mesh(devices.reshape(-1, group), DP)
    rows = P(DP, None)
    placed = (rows, rows, rows, rows, rows, P(), rows)
    return jax.shard_map(
        local,
        mesh=pair_mesh,
        in_specs=placed,
        out_specs=(rows, rows, rows, rows),
        check_vma=False,
    )
```

```python
import math

import jax
import jax.numpy as jnp
from jax import lax
from jax.sharding import Mesh, PartitionSpec as P
import numpy as np
from jax.experimental import pallas as pl
from jax.experimental.pallas import tpu as pltpu

HQ = 16
HK = 4
DH = 128
INTERPRET = False


NT = (((1,), (1,)), ((), ()))
TN = (((0,), (0,)), ((), ()))


def attend_kernel(
    seg_col_ref, seg_row_ref, key_col_ref, key_row_ref, q_ref, k_ref, v_ref, o_ref, out_ref
):
    row_count = q_ref.shape[0]
    group_size = HQ // HK
    q_w = group_size * DH
    score_scale = 1.0 / math.sqrt(DH)
    seg_col = seg_col_ref[...]
    live_rows = seg_col >= 0
    allowed = (
        (seg_col == seg_row_ref[...]) & (key_row_ref[...] <= key_col_ref[...]) & live_rows
    )
    k_group = k_ref[...]
    v_group = v_ref[...]
    dk_acc = jnp.zeros((row_count, DH), jnp.float32)
    dv_acc = jnp.zeros((row_count, DH), jnp.float32)
    for head in range(group_size):
        q_head = q_ref[:, head * DH : (head + 1) * DH]
        o_head = o_ref[:, head * DH : (head + 1) * DH]
        scores = lax.dot_general(q_head, k_group, NT, preferred_element_type=jnp.float32)
        scores = jnp.where(allowed, scores * score_scale, jnp.float32(-1000000000.0))
        row_max = jnp.max(scores, axis=1, keepdims=True)
        weights = jnp.exp(scores - row_max)
        attn_probs = weights * (1.0 / jnp.sum(weights, axis=1, keepdims=True))
        attn_probs = jnp.where(live_rows, attn_probs, jnp.float32(0.0))
        probs_b = attn_probs.astype(jnp.bfloat16)
        dv_acc = dv_acc + lax.dot_general(probs_b, o_head, TN, preferred_element_type=jnp.float32)
        dprob = lax.dot_general(o_head, v_group, NT, preferred_element_type=jnp.float32)
        row_delta = jnp.sum(attn_probs * dprob, axis=1, keepdims=True)
        dscore = (attn_probs * (dprob - row_delta) * score_scale).astype(jnp.bfloat16)
        out_ref[:, head * DH : (head + 1) * DH] = jnp.dot(
            dscore, k_group, preferred_element_type=jnp.float32
        ).astype(out_ref.dtype)
        dk_acc = dk_acc + lax.dot_general(dscore, q_head, TN, preferred_element_type=jnp.float32)
    out_ref[:, q_w : q_w + DH] = dk_acc.astype(out_ref.dtype)
    out_ref[:, q_w + DH : q_w + 2 * DH] = dv_acc.astype(out_ref.dtype)


def attend_rows(rows_in, segment, order_key):
    row_count = rows_in.shape[0]
    q_w = (HQ // HK) * DH
    out_w = q_w + 2 * DH
    k_at, v_at, o_at = HK * q_w // DH, HK * q_w // DH + HK, (HK * q_w + 2 * HK * DH) // q_w
    whole = lambda g: (0, 0)
    col = pl.BlockSpec((row_count, 1), whole)
    row = pl.BlockSpec((1, row_count), whole)
    return pl.pallas_call(
        attend_kernel,
        grid=(HK,),
        in_specs=[
            col,
            row,
            col,
            row,
            pl.BlockSpec((row_count, q_w), lambda g: (0, g)),
            pl.BlockSpec((row_count, DH), lambda g: (0, k_at + g)),
            pl.BlockSpec((row_count, DH), lambda g: (0, v_at + g)),
            pl.BlockSpec((row_count, q_w), lambda g: (0, o_at + g)),
        ],
        out_specs=pl.BlockSpec((row_count, out_w), lambda g: (0, g)),
        out_shape=jax.ShapeDtypeStruct((row_count, HK * out_w), jnp.bfloat16),
        compiler_params=pltpu.CompilerParams(dimension_semantics=("arbitrary",)),
        interpret=INTERPRET,
    )(
        segment.reshape(row_count, 1),
        segment.reshape(1, row_count),
        order_key.reshape(row_count, 1),
        order_key.reshape(1, row_count),
        rows_in,
        rows_in,
        rows_in,
        rows_in,
    )


OUTER, INNER = "outer", "inner"
DP = (OUTER, INNER)
GROUP = 8


def local(hidden_in, queries, keys, values, grad_attn, send_rows, slot_docs):
    outers, groups = lax.axis_size(OUTER), lax.axis_size(INNER)
    owners = outers * groups
    slot_count = send_rows.shape[0]
    tok_rows = queries.shape[0]
    group_size = HQ // HK
    q_w = group_size * DH
    live_send = (send_rows >= 0).T
    pick_rows = jnp.maximum(send_rows, 0).T
    grad_scale = 1.0 / math.sqrt(tok_rows * owners)
    table = jnp.concatenate((queries, keys, values, grad_attn), axis=1)
    rows_in = lax.all_to_all(table[pick_rows], DP, 0, 0, tiled=True)
    rows_in = rows_in.reshape(owners * slot_count, table.shape[1])
    row_ids = jnp.arange(owners * slot_count, dtype=jnp.int32)
    order_key = (row_ids % slot_count) * owners + row_ids // slot_count
    segment = jnp.tile(slot_docs[0].astype(jnp.int32), owners)
    rows_out = attend_rows(rows_in, segment, order_key)
    back = lax.all_to_all(
        rows_out.reshape(owners, slot_count, rows_out.shape[1]), DP, 0, 0, tiled=True
    )
    targets = jnp.where(live_send, pick_rows, tok_rows).reshape(-1)
    home = (
        jnp.zeros((tok_rows, back.shape[2]), back.dtype)
        .at[targets]
        .set(back.reshape(owners * slot_count, back.shape[2]), mode="drop")
    )
    out_w = q_w + 2 * DH
    grad_queries = jnp.concatenate(
        [home[:, g * out_w : g * out_w + q_w] for g in range(HK)], axis=1
    )
    grad_keys = jnp.concatenate(
        [home[:, g * out_w + q_w : g * out_w + q_w + DH] for g in range(HK)], axis=1
    )
    grad_values = jnp.concatenate(
        [home[:, g * out_w + q_w + DH : (g + 1) * out_w] for g in range(HK)], axis=1
    )
    me = lax.axis_index(INNER)
    shifts = range(1, groups)
    blocks = hidden_in.reshape(tok_rows, outers, groups, -1)
    hidden_grp = [lax.dynamic_index_in_dim(blocks, me, axis=2, keepdims=False)]
    for shift in shifts:
        ring = [(i, (i + shift) % groups) for i in range(groups)]
        theirs = lax.dynamic_index_in_dim(blocks, (me + shift) % groups, axis=2, keepdims=False)
        hidden_grp.append(lax.ppermute(theirs, INNER, ring))
    hidden_grp = jnp.concatenate(hidden_grp, axis=0).reshape(groups * tok_rows, -1)
    spread = jnp.broadcast_to(grad_values[None], (groups,) + grad_values.shape)
    gathered = lax.all_to_all(spread, INNER, 0, 0, tiled=True)
    order = (me - jnp.arange(groups, dtype=jnp.int32)) % groups
    grad_grp = jnp.take(gathered, order, axis=0).reshape(groups * tok_rows, -1)
    partial = jnp.einsum("td,tc->dc", hidden_grp, grad_grp, preferred_element_type=jnp.float32)
    partial = partial.reshape(outers, partial.shape[0] // outers, partial.shape[1])
    grad_wv = lax.all_to_all(partial, OUTER, 0, 0, tiled=True).sum(0) * grad_scale
    return (grad_queries, grad_keys, grad_values, grad_wv)


def solution(mesh):
    devices = np.asarray(mesh.devices).reshape(-1)
    group = GROUP if devices.size % GROUP == 0 else 1
    pair_mesh = Mesh(devices.reshape(-1, group), DP)
    rows = P(DP, None)
    placed = (rows, rows, rows, rows, rows, P(), rows)
    return jax.shard_map(
        local,
        mesh=pair_mesh,
        in_specs=placed,
        out_specs=(rows, rows, rows, rows),
        check_vma=False,
    )
```

```python
import math

import jax
import jax.numpy as jnp
from jax import lax
from jax.sharding import Mesh, PartitionSpec as P
import numpy as np
from jax.experimental import pallas as pl
from jax.experimental.pallas import tpu as pltpu

HQ = 16
HK = 4
DH = 128
INTERPRET = False


NT = (((1,), (1,)), ((), ()))
TN = (((0,), (0,)), ((), ()))


def attend_kernel(
    seg_col_ref, seg_row_ref, key_col_ref, key_row_ref, q_ref, k_ref, v_ref, o_ref, out_ref
):
    row_count = q_ref.shape[0]
    group_size = HQ // HK
    q_w = group_size * DH
    score_scale = 1.0 / math.sqrt(DH)
    seg_col = seg_col_ref[...]
    live_rows = seg_col >= 0
    allowed = (
        (seg_col == seg_row_ref[...]) & (key_row_ref[...] <= key_col_ref[...]) & live_rows
    )
    k_group = k_ref[...]
    v_group = v_ref[...]
    dk_acc = jnp.zeros((row_count, DH), jnp.float32)
    dv_acc = jnp.zeros((row_count, DH), jnp.float32)
    for head in range(group_size):
        q_head = q_ref[:, head * DH : (head + 1) * DH]
        o_head = o_ref[:, head * DH : (head + 1) * DH]
        scores = lax.dot_general(q_head, k_group, NT, preferred_element_type=jnp.float32)
        scores = jnp.where(allowed, scores * score_scale, jnp.float32(-1000000000.0))
        row_max = jnp.max(scores, axis=1, keepdims=True)
        weights = jnp.exp(scores - row_max)
        attn_probs = weights * (1.0 / jnp.sum(weights, axis=1, keepdims=True))
        attn_probs = jnp.where(live_rows, attn_probs, jnp.float32(0.0))
        probs_b = attn_probs.astype(jnp.bfloat16)
        dv_acc = dv_acc + lax.dot_general(probs_b, o_head, TN, preferred_element_type=jnp.float32)
        dprob = lax.dot_general(o_head, v_group, NT, preferred_element_type=jnp.float32)
        row_delta = jnp.sum(attn_probs * dprob, axis=1, keepdims=True)
        dscore = (attn_probs * (dprob - row_delta) * score_scale).astype(jnp.bfloat16)
        out_ref[:, head * DH : (head + 1) * DH] = jnp.dot(
            dscore, k_group, preferred_element_type=jnp.float32
        ).astype(out_ref.dtype)
        dk_acc = dk_acc + lax.dot_general(dscore, q_head, TN, preferred_element_type=jnp.float32)
    out_ref[:, q_w : q_w + DH] = dk_acc.astype(out_ref.dtype)
    out_ref[:, q_w + DH : q_w + 2 * DH] = dv_acc.astype(out_ref.dtype)


def attend_rows(rows_in, segment, order_key):
    row_count = rows_in.shape[0]
    q_w = (HQ // HK) * DH
    out_w = q_w + 2 * DH
    k_at, v_at, o_at = HK * q_w // DH, HK * q_w // DH + HK, (HK * q_w + 2 * HK * DH) // q_w
    whole = lambda g: (0, 0)
    col = pl.BlockSpec((row_count, 1), whole)
    row = pl.BlockSpec((1, row_count), whole)
    return pl.pallas_call(
        attend_kernel,
        grid=(HK,),
        in_specs=[
            col,
            row,
            col,
            row,
            pl.BlockSpec((row_count, q_w), lambda g: (0, g)),
            pl.BlockSpec((row_count, DH), lambda g: (0, k_at + g)),
            pl.BlockSpec((row_count, DH), lambda g: (0, v_at + g)),
            pl.BlockSpec((row_count, q_w), lambda g: (0, o_at + g)),
        ],
        out_specs=pl.BlockSpec((row_count, out_w), lambda g: (0, g)),
        out_shape=jax.ShapeDtypeStruct((row_count, HK * out_w), jnp.bfloat16),
        compiler_params=pltpu.CompilerParams(dimension_semantics=("arbitrary",)),
        interpret=INTERPRET,
    )(
        segment.reshape(row_count, 1),
        segment.reshape(1, row_count),
        order_key.reshape(row_count, 1),
        order_key.reshape(1, row_count),
        rows_in,
        rows_in,
        rows_in,
        rows_in,
    )


OUTER, INNER = "outer", "inner"
DP = (OUTER, INNER)
GROUP = 8


def local(hidden_in, queries, keys, values, grad_attn, send_rows, slot_docs):
    outers, groups = lax.axis_size(OUTER), lax.axis_size(INNER)
    owners = outers * groups
    slot_count = send_rows.shape[0]
    tok_rows = queries.shape[0]
    group_size = HQ // HK
    q_w = group_size * DH
    live_send = (send_rows >= 0).T
    pick_rows = jnp.maximum(send_rows, 0).T
    grad_scale = 1.0 / math.sqrt(tok_rows * owners)
    table = jnp.concatenate((queries, keys, values, grad_attn), axis=1)
    me = lax.axis_index(INNER)
    shifts = range(1, groups)
    blocks = hidden_in.reshape(tok_rows, outers, groups, -1)
    hidden_grp = [lax.dynamic_index_in_dim(blocks, me, axis=2, keepdims=False)]
    for shift in shifts:
        ring = [(i, (i + shift) % groups) for i in range(groups)]
        theirs = lax.dynamic_index_in_dim(blocks, (me + shift) % groups, axis=2, keepdims=False)
        hidden_grp.append(lax.ppermute(theirs, INNER, ring))
    hidden_grp = jnp.concatenate(hidden_grp, axis=0).reshape(groups * tok_rows, -1)
    rows_in = lax.all_to_all(table[pick_rows], DP, 0, 0, tiled=True)
    rows_in = rows_in.reshape(owners * slot_count, table.shape[1])
    row_ids = jnp.arange(owners * slot_count, dtype=jnp.int32)
    order_key = (row_ids % slot_count) * owners + row_ids // slot_count
    segment = jnp.tile(slot_docs[0].astype(jnp.int32), owners)
    hidden_grp, rows_in = lax.optimization_barrier((hidden_grp, rows_in))
    rows_out = attend_rows(rows_in, segment, order_key)
    back = lax.all_to_all(
        rows_out.reshape(owners, slot_count, rows_out.shape[1]), DP, 0, 0, tiled=True
    )
    targets = jnp.where(live_send, pick_rows, tok_rows).reshape(-1)
    home = (
        jnp.zeros((tok_rows, back.shape[2]), back.dtype)
        .at[targets]
        .set(back.reshape(owners * slot_count, back.shape[2]), mode="drop")
    )
    out_w = q_w + 2 * DH
    grad_queries = jnp.concatenate(
        [home[:, g * out_w : g * out_w + q_w] for g in range(HK)], axis=1
    )
    grad_keys = jnp.concatenate(
        [home[:, g * out_w + q_w : g * out_w + q_w + DH] for g in range(HK)], axis=1
    )
    grad_values = jnp.concatenate(
        [home[:, g * out_w + q_w + DH : (g + 1) * out_w] for g in range(HK)], axis=1
    )
    spread = jnp.broadcast_to(grad_values[None], (groups,) + grad_values.shape)
    gathered = lax.all_to_all(spread, INNER, 0, 0, tiled=True)
    order = (me - jnp.arange(groups, dtype=jnp.int32)) % groups
    grad_grp = jnp.take(gathered, order, axis=0).reshape(groups * tok_rows, -1)
    partial = jnp.einsum("td,tc->dc", hidden_grp, grad_grp, preferred_element_type=jnp.float32)
    partial = partial.reshape(outers, partial.shape[0] // outers, partial.shape[1])
    grad_wv = lax.all_to_all(partial, OUTER, 0, 0, tiled=True).sum(0) * grad_scale
    return (grad_queries, grad_keys, grad_values, grad_wv)


def solution(mesh):
    devices = np.asarray(mesh.devices).reshape(-1)
    group = GROUP if devices.size % GROUP == 0 else 1
    pair_mesh = Mesh(devices.reshape(-1, group), DP)
    rows = P(DP, None)
    placed = (rows, rows, rows, rows, rows, P(), rows)
    return jax.shard_map(
        local,
        mesh=pair_mesh,
        in_specs=placed,
        out_specs=(rows, rows, rows, rows),
        check_vma=False,
    )
```

```python
import math

import jax
import jax.numpy as jnp
from jax import lax
from jax.sharding import Mesh, PartitionSpec as P
import numpy as np
from jax.experimental import pallas as pl
from jax.experimental.pallas import tpu as pltpu

HQ = 16
HK = 4
DH = 128
INTERPRET = False


NT = (((1,), (1,)), ((), ()))
TN = (((0,), (0,)), ((), ()))


def attend_kernel(
    seg_col_ref, seg_row_ref, key_col_ref, key_row_ref, q_ref, k_ref, v_ref, o_ref, out_ref
):
    row_count = q_ref.shape[0]
    group_size = HQ // HK
    q_w = group_size * DH
    score_scale = 1.0 / math.sqrt(DH)
    seg_row = seg_row_ref[...]
    live_queries = seg_row >= 0
    allowed = (
        (seg_col_ref[...] == seg_row) & (key_col_ref[...] <= key_row_ref[...]) & live_queries
    )
    k_group = k_ref[...]
    v_group = v_ref[...]
    dk_acc = jnp.zeros((row_count, DH), jnp.float32)
    dv_acc = jnp.zeros((row_count, DH), jnp.float32)
    for head in range(group_size):
        q_head = q_ref[:, head * DH : (head + 1) * DH]
        o_head = o_ref[:, head * DH : (head + 1) * DH]
        scores = lax.dot_general(k_group, q_head, NT, preferred_element_type=jnp.float32)
        scores = jnp.where(allowed, scores * score_scale, jnp.float32(-1000000000.0))
        col_max = jnp.max(scores, axis=0, keepdims=True)
        weights = jnp.exp(scores - col_max)
        scale_of = jnp.where(
            live_queries, 1.0 / jnp.sum(weights, axis=0, keepdims=True), jnp.float32(0.0)
        )
        attn_probs = weights * scale_of
        dv_acc = dv_acc + jnp.dot(
            attn_probs.astype(jnp.bfloat16), o_head, preferred_element_type=jnp.float32
        )
        dprob = lax.dot_general(v_group, o_head, NT, preferred_element_type=jnp.float32)
        row_delta = jnp.sum(attn_probs * dprob, axis=0, keepdims=True)
        dscore = (attn_probs * (dprob - row_delta) * score_scale).astype(jnp.bfloat16)
        out_ref[:, head * DH : (head + 1) * DH] = lax.dot_general(
            dscore, k_group, TN, preferred_element_type=jnp.float32
        ).astype(out_ref.dtype)
        dk_acc = dk_acc + jnp.dot(dscore, q_head, preferred_element_type=jnp.float32)
    out_ref[:, q_w : q_w + DH] = dk_acc.astype(out_ref.dtype)
    out_ref[:, q_w + DH : q_w + 2 * DH] = dv_acc.astype(out_ref.dtype)


def attend_rows(rows_in, segment, order_key):
    row_count = rows_in.shape[0]
    q_w = (HQ // HK) * DH
    out_w = q_w + 2 * DH
    k_at, v_at, o_at = HK * q_w // DH, HK * q_w // DH + HK, (HK * q_w + 2 * HK * DH) // q_w
    whole = lambda g: (0, 0)
    col = pl.BlockSpec((row_count, 1), whole)
    row = pl.BlockSpec((1, row_count), whole)
    return pl.pallas_call(
        attend_kernel,
        grid=(HK,),
        in_specs=[
            col,
            row,
            col,
            row,
            pl.BlockSpec((row_count, q_w), lambda g: (0, g)),
            pl.BlockSpec((row_count, DH), lambda g: (0, k_at + g)),
            pl.BlockSpec((row_count, DH), lambda g: (0, v_at + g)),
            pl.BlockSpec((row_count, q_w), lambda g: (0, o_at + g)),
        ],
        out_specs=pl.BlockSpec((row_count, out_w), lambda g: (0, g)),
        out_shape=jax.ShapeDtypeStruct((row_count, HK * out_w), jnp.bfloat16),
        compiler_params=pltpu.CompilerParams(dimension_semantics=("arbitrary",)),
        interpret=INTERPRET,
    )(
        segment.reshape(row_count, 1),
        segment.reshape(1, row_count),
        order_key.reshape(row_count, 1),
        order_key.reshape(1, row_count),
        rows_in,
        rows_in,
        rows_in,
        rows_in,
    )


CHIP, CORE = "chip", "core"
DP = (CHIP, CORE)


def local(hidden_in, queries, keys, values, grad_attn, send_rows, slot_docs):
    chips, cores = lax.axis_size(CHIP), lax.axis_size(CORE)
    owners = chips * cores
    slot_count = send_rows.shape[0]
    tok_rows = queries.shape[0]
    group_size = HQ // HK
    q_w = group_size * DH
    live_send = (send_rows >= 0).T
    pick_rows = jnp.maximum(send_rows, 0).T
    grad_scale = 1.0 / math.sqrt(tok_rows * owners)
    table = jnp.concatenate((queries, keys, values, grad_attn), axis=1)
    rows_in = lax.all_to_all(table[pick_rows], DP, 0, 0, tiled=True)
    rows_in = rows_in.reshape(owners * slot_count, table.shape[1])
    row_ids = jnp.arange(owners * slot_count, dtype=jnp.int32)
    order_key = (row_ids % slot_count) * owners + row_ids // slot_count
    segment = jnp.tile(slot_docs[0].astype(jnp.int32), owners)
    rows_out = attend_rows(rows_in, segment, order_key)
    back = lax.all_to_all(
        rows_out.reshape(owners, slot_count, rows_out.shape[1]), DP, 0, 0, tiled=True
    )
    targets = jnp.where(live_send, pick_rows, tok_rows).reshape(-1)
    home = (
        jnp.zeros((tok_rows, back.shape[2]), back.dtype)
        .at[targets]
        .set(back.reshape(owners * slot_count, back.shape[2]), mode="drop")
    )
    out_w = q_w + 2 * DH
    grad_queries = jnp.concatenate(
        [home[:, g * out_w : g * out_w + q_w] for g in range(HK)], axis=1
    )
    grad_keys = jnp.concatenate(
        [home[:, g * out_w + q_w : g * out_w + q_w + DH] for g in range(HK)], axis=1
    )
    grad_values = jnp.concatenate(
        [home[:, g * out_w + q_w + DH : (g + 1) * out_w] for g in range(HK)], axis=1
    )
    core = lax.axis_index(CORE)
    swap = [(0, 1), (1, 0)]
    blocks = hidden_in.reshape(tok_rows, chips, cores, -1)
    mine = lax.dynamic_index_in_dim(blocks, core, axis=2, keepdims=False)
    theirs = lax.dynamic_index_in_dim(blocks, 1 - core, axis=2, keepdims=False)
    from_partner = lax.ppermute(theirs, CORE, swap)
    hidden_pair = jnp.concatenate((mine, from_partner), axis=0).reshape(2 * tok_rows, -1)
    grad_pair = jnp.concatenate((grad_values, lax.ppermute(grad_values, CORE, swap)), axis=0)
    partial = jnp.einsum("td,tc->dc", hidden_pair, grad_pair, preferred_element_type=jnp.float32)
    partial = partial.reshape(chips, partial.shape[0] // chips, partial.shape[1])
    grad_wv = lax.all_to_all(partial, CHIP, 0, 0, tiled=True).sum(0) * grad_scale
    return (grad_queries, grad_keys, grad_values, grad_wv)


def solution(mesh):
    devices = np.asarray(mesh.devices).reshape(-1)
    pair_mesh = Mesh(devices.reshape(-1, 2), DP)
    rows = P(DP, None)
    placed = (rows, rows, rows, rows, rows, P(), rows)
    return jax.shard_map(
        local,
        mesh=pair_mesh,
        in_specs=placed,
        out_specs=(rows, rows, rows, rows),
        check_vma=False,
    )
```

```python
import math

import jax
import jax.numpy as jnp
from jax import lax
from jax.sharding import Mesh, PartitionSpec as P
import numpy as np
from jax.experimental import pallas as pl
from jax.experimental.pallas import tpu as pltpu

HQ = 16
HK = 4
DH = 128
INTERPRET = False


NT = (((1,), (1,)), ((), ()))
TN = (((0,), (0,)), ((), ()))


def attend_kernel(
    seg_col_ref, seg_row_ref, key_col_ref, key_row_ref, q_ref, k_ref, v_ref, o_ref, out_ref
):
    row_count = q_ref.shape[0]
    group_size = HQ // HK
    q_w = group_size * DH
    score_scale = 1.0 / math.sqrt(DH)
    seg_row = seg_row_ref[...]
    live_queries = seg_row >= 0
    allowed = (
        (seg_col_ref[...] == seg_row) & (key_col_ref[...] <= key_row_ref[...]) & live_queries
    )
    k_group = k_ref[...]
    v_group = v_ref[...]
    dk_acc = jnp.zeros((row_count, DH), jnp.float32)
    dv_acc = jnp.zeros((row_count, DH), jnp.float32)
    for head in range(group_size):
        q_head = q_ref[:, head * DH : (head + 1) * DH]
        o_head = o_ref[:, head * DH : (head + 1) * DH]
        scores = lax.dot_general(k_group, q_head, NT, preferred_element_type=jnp.float32)
        scores = jnp.where(allowed, scores * score_scale, jnp.float32(-1000000000.0))
        col_max = jnp.max(scores, axis=0, keepdims=True)
        weights = jnp.exp(scores - col_max)
        scale_of = jnp.where(
            live_queries, 1.0 / jnp.sum(weights, axis=0, keepdims=True), jnp.float32(0.0)
        )
        attn_probs = weights * scale_of
        dv_acc = dv_acc + jnp.dot(
            attn_probs.astype(jnp.bfloat16), o_head, preferred_element_type=jnp.float32
        )
        dprob = lax.dot_general(v_group, o_head, NT, preferred_element_type=jnp.float32)
        row_delta = jnp.sum(attn_probs * dprob, axis=0, keepdims=True)
        dscore = (attn_probs * (dprob - row_delta) * score_scale).astype(jnp.bfloat16)
        out_ref[:, head * DH : (head + 1) * DH] = lax.dot_general(
            dscore, k_group, TN, preferred_element_type=jnp.float32
        ).astype(out_ref.dtype)
        dk_acc = dk_acc + jnp.dot(dscore, q_head, preferred_element_type=jnp.float32)
    out_ref[:, q_w : q_w + DH] = dk_acc.astype(out_ref.dtype)
    out_ref[:, q_w + DH : q_w + 2 * DH] = dv_acc.astype(out_ref.dtype)


def attend_rows(rows_in, segment, order_key):
    row_count = rows_in.shape[0]
    q_w = (HQ // HK) * DH
    out_w = q_w + 2 * DH
    k_at, v_at, o_at = HK * q_w // DH, HK * q_w // DH + HK, (HK * q_w + 2 * HK * DH) // q_w
    whole = lambda g: (0, 0)
    col = pl.BlockSpec((row_count, 1), whole)
    row = pl.BlockSpec((1, row_count), whole)
    return pl.pallas_call(
        attend_kernel,
        grid=(HK,),
        in_specs=[
            col,
            row,
            col,
            row,
            pl.BlockSpec((row_count, q_w), lambda g: (0, g)),
            pl.BlockSpec((row_count, DH), lambda g: (0, k_at + g)),
            pl.BlockSpec((row_count, DH), lambda g: (0, v_at + g)),
            pl.BlockSpec((row_count, q_w), lambda g: (0, o_at + g)),
        ],
        out_specs=pl.BlockSpec((row_count, out_w), lambda g: (0, g)),
        out_shape=jax.ShapeDtypeStruct((row_count, HK * out_w), jnp.bfloat16),
        compiler_params=pltpu.CompilerParams(dimension_semantics=("arbitrary",)),
        interpret=INTERPRET,
    )(
        segment.reshape(row_count, 1),
        segment.reshape(1, row_count),
        order_key.reshape(row_count, 1),
        order_key.reshape(1, row_count),
        rows_in,
        rows_in,
        rows_in,
        rows_in,
    )


CHIP, CORE = "chip", "core"
DP = (CHIP, CORE)


def local(hidden_in, queries, keys, values, grad_attn, send_rows, slot_docs):
    chips, cores = lax.axis_size(CHIP), lax.axis_size(CORE)
    owners = chips * cores
    slot_count = send_rows.shape[0]
    tok_rows = queries.shape[0]
    group_size = HQ // HK
    q_w = group_size * DH
    live_send = (send_rows >= 0).T
    pick_rows = jnp.maximum(send_rows, 0).T
    grad_scale = 1.0 / math.sqrt(tok_rows * owners)
    table = jnp.concatenate((queries, keys, values, grad_attn), axis=1)
    rows_in = lax.all_to_all(table[pick_rows], DP, 0, 0, tiled=True)
    rows_in = rows_in.reshape(owners * slot_count, table.shape[1])
    row_ids = jnp.arange(owners * slot_count, dtype=jnp.int32)
    order_key = (row_ids % slot_count) * owners + row_ids // slot_count
    segment = jnp.tile(slot_docs[0].astype(jnp.int32), owners)
    rows_out = attend_rows(rows_in, segment, order_key)
    back = lax.all_to_all(
        rows_out.reshape(owners, slot_count, rows_out.shape[1]), DP, 0, 0, tiled=True
    )
    targets = jnp.where(live_send, pick_rows, tok_rows).reshape(-1)
    slot_of_row = (
        jnp.zeros((tok_rows,), jnp.int32)
        .at[targets]
        .set(jnp.arange(owners * slot_count, dtype=jnp.int32), mode="drop")
    )
    home = back.reshape(owners * slot_count, back.shape[2])[slot_of_row]
    out_w = q_w + 2 * DH
    grad_queries = jnp.concatenate(
        [home[:, g * out_w : g * out_w + q_w] for g in range(HK)], axis=1
    )
    grad_keys = jnp.concatenate(
        [home[:, g * out_w + q_w : g * out_w + q_w + DH] for g in range(HK)], axis=1
    )
    grad_values = jnp.concatenate(
        [home[:, g * out_w + q_w + DH : (g + 1) * out_w] for g in range(HK)], axis=1
    )
    core = lax.axis_index(CORE)
    swap = [(0, 1), (1, 0)]
    blocks = hidden_in.reshape(tok_rows, chips, cores, -1)
    mine = lax.dynamic_index_in_dim(blocks, core, axis=2, keepdims=False)
    theirs = lax.dynamic_index_in_dim(blocks, 1 - core, axis=2, keepdims=False)
    from_partner = lax.ppermute(theirs, CORE, swap)
    hidden_pair = jnp.concatenate((mine, from_partner), axis=0).reshape(2 * tok_rows, -1)
    grad_pair = jnp.concatenate((grad_values, lax.ppermute(grad_values, CORE, swap)), axis=0)
    partial = jnp.einsum("td,tc->dc", hidden_pair, grad_pair, preferred_element_type=jnp.float32)
    partial = partial.reshape(chips, partial.shape[0] // chips, partial.shape[1])
    grad_wv = lax.all_to_all(partial, CHIP, 0, 0, tiled=True).sum(0) * grad_scale
    return (grad_queries, grad_keys, grad_values, grad_wv)


def solution(mesh):
    devices = np.asarray(mesh.devices).reshape(-1)
    pair_mesh = Mesh(devices.reshape(-1, 2), DP)
    rows = P(DP, None)
    placed = (rows, rows, rows, rows, rows, P(), rows)
    return jax.shard_map(
        local,
        mesh=pair_mesh,
        in_specs=placed,
        out_specs=(rows, rows, rows, rows),
        check_vma=False,
    )
```

```python
import math

import jax
import jax.numpy as jnp
from jax import lax
from jax.sharding import Mesh, PartitionSpec as P
import numpy as np
from jax.experimental import pallas as pl
from jax.experimental.pallas import tpu as pltpu

HQ = 16
HK = 4
DH = 128
INTERPRET = False


NT = (((1,), (1,)), ((), ()))
TN = (((0,), (0,)), ((), ()))


def attend_kernel(
    seg_col_ref, seg_row_ref, key_col_ref, key_row_ref, q_ref, k_ref, v_ref, o_ref, out_ref
):
    row_count = q_ref.shape[0]
    group_size = HQ // HK
    q_w = group_size * DH
    score_scale = 1.0 / math.sqrt(DH)
    seg_row = seg_row_ref[...]
    live_queries = seg_row >= 0
    allowed = (
        (seg_col_ref[...] == seg_row) & (key_col_ref[...] <= key_row_ref[...]) & live_queries
    )
    k_group = k_ref[...]
    v_group = v_ref[...]
    dk_acc = jnp.zeros((row_count, DH), jnp.float32)
    dv_acc = jnp.zeros((row_count, DH), jnp.float32)
    for head in range(group_size):
        q_head = q_ref[:, head * DH : (head + 1) * DH]
        o_head = o_ref[:, head * DH : (head + 1) * DH]
        scores = lax.dot_general(k_group, q_head, NT, preferred_element_type=jnp.float32)
        scores = jnp.where(allowed, scores * score_scale, jnp.float32(-1000000000.0))
        col_max = jnp.max(scores, axis=0, keepdims=True)
        weights = jnp.exp(scores - col_max)
        scale_of = jnp.where(
            live_queries, 1.0 / jnp.sum(weights, axis=0, keepdims=True), jnp.float32(0.0)
        )
        attn_probs = weights * scale_of
        dv_acc = dv_acc + jnp.dot(
            attn_probs.astype(jnp.bfloat16), o_head, preferred_element_type=jnp.float32
        )
        dprob = lax.dot_general(v_group, o_head, NT, preferred_element_type=jnp.float32)
        row_delta = jnp.sum(attn_probs * dprob, axis=0, keepdims=True)
        dscore = (attn_probs * (dprob - row_delta) * score_scale).astype(jnp.bfloat16)
        out_ref[:, head * DH : (head + 1) * DH] = lax.dot_general(
            dscore, k_group, TN, preferred_element_type=jnp.float32
        ).astype(out_ref.dtype)
        dk_acc = dk_acc + jnp.dot(dscore, q_head, preferred_element_type=jnp.float32)
    out_ref[:, q_w : q_w + DH] = dk_acc.astype(out_ref.dtype)
    out_ref[:, q_w + DH : q_w + 2 * DH] = dv_acc.astype(out_ref.dtype)


def attend_rows(rows_in, segment, order_key, n_kv):
    row_count = rows_in.shape[0]
    q_w = (HQ // HK) * DH
    out_w = q_w + 2 * DH
    k_at, v_at, o_at = n_kv * q_w // DH, n_kv * q_w // DH + n_kv, (n_kv + 2 * n_kv * DH // q_w)
    whole = lambda g: (0, 0)
    col = pl.BlockSpec((row_count, 1), whole)
    row = pl.BlockSpec((1, row_count), whole)
    return pl.pallas_call(
        attend_kernel,
        grid=(n_kv,),
        in_specs=[
            col,
            row,
            col,
            row,
            pl.BlockSpec((row_count, q_w), lambda g: (0, g)),
            pl.BlockSpec((row_count, DH), lambda g: (0, k_at + g)),
            pl.BlockSpec((row_count, DH), lambda g: (0, v_at + g)),
            pl.BlockSpec((row_count, q_w), lambda g: (0, o_at + g)),
        ],
        out_specs=pl.BlockSpec((row_count, out_w), lambda g: (0, g)),
        out_shape=jax.ShapeDtypeStruct((row_count, n_kv * out_w), jnp.bfloat16),
        compiler_params=pltpu.CompilerParams(dimension_semantics=("arbitrary",)),
        interpret=INTERPRET,
    )(
        segment.reshape(row_count, 1),
        segment.reshape(1, row_count),
        order_key.reshape(row_count, 1),
        order_key.reshape(1, row_count),
        rows_in,
        rows_in,
        rows_in,
        rows_in,
    )


CHIP, CORE = "chip", "core"
DP = (CHIP, CORE)
PARTS = 2


def local(hidden_in, queries, keys, values, grad_attn, send_rows, slot_docs):
    chips, cores = lax.axis_size(CHIP), lax.axis_size(CORE)
    owners = chips * cores
    slot_count = send_rows.shape[0]
    tok_rows = queries.shape[0]
    group_size = HQ // HK
    q_w = group_size * DH
    live_send = (send_rows >= 0).T
    pick_rows = jnp.maximum(send_rows, 0).T
    grad_scale = 1.0 / math.sqrt(tok_rows * owners)
    row_ids = jnp.arange(owners * slot_count, dtype=jnp.int32)
    order_key = (row_ids % slot_count) * owners + row_ids // slot_count
    segment = jnp.tile(slot_docs[0].astype(jnp.int32), owners)
    targets = jnp.where(live_send, pick_rows, tok_rows).reshape(-1)
    out_w = q_w + 2 * DH
    core = lax.axis_index(CORE)
    swap = [(0, 1), (1, 0)]
    blocks = hidden_in.reshape(tok_rows, chips, cores, -1)
    mine = lax.dynamic_index_in_dim(blocks, core, axis=2, keepdims=False)
    theirs = lax.dynamic_index_in_dim(blocks, 1 - core, axis=2, keepdims=False)
    from_partner = lax.ppermute(theirs, CORE, swap)
    hidden_pair = jnp.concatenate((mine, from_partner), axis=0).reshape(2 * tok_rows, -1)
    n_kv = HK // PARTS
    dq_parts, dk_parts, dv_parts, wv_parts = [], [], [], []
    for part in range(PARTS):
        q_cols = slice(part * n_kv * q_w, (part + 1) * n_kv * q_w)
        kv_cols = slice(part * n_kv * DH, (part + 1) * n_kv * DH)
        table = jnp.concatenate(
            (queries[:, q_cols], keys[:, kv_cols], values[:, kv_cols], grad_attn[:, q_cols]), axis=1
        )
        rows_in = lax.all_to_all(table[pick_rows], DP, 0, 0, tiled=True)
        rows_in = rows_in.reshape(owners * slot_count, table.shape[1])
        rows_out = attend_rows(rows_in, segment, order_key, n_kv)
        back = lax.all_to_all(
            rows_out.reshape(owners, slot_count, rows_out.shape[1]), DP, 0, 0, tiled=True
        )
        home = (
            jnp.zeros((tok_rows, back.shape[2]), back.dtype)
            .at[targets]
            .set(back.reshape(owners * slot_count, back.shape[2]), mode="drop")
        )
        dq_parts += [home[:, g * out_w : g * out_w + q_w] for g in range(n_kv)]
        dk_parts += [home[:, g * out_w + q_w : g * out_w + q_w + DH] for g in range(n_kv)]
        dv_part = jnp.concatenate(
            [home[:, g * out_w + q_w + DH : (g + 1) * out_w] for g in range(n_kv)], axis=1
        )
        dv_parts.append(dv_part)
        grad_pair = jnp.concatenate((dv_part, lax.ppermute(dv_part, CORE, swap)), axis=0)
        partial = jnp.einsum(
            "td,tc->dc", hidden_pair, grad_pair, preferred_element_type=jnp.float32
        )
        partial = partial.reshape(chips, partial.shape[0] // chips, partial.shape[1])
        wv_parts.append(lax.all_to_all(partial, CHIP, 0, 0, tiled=True).sum(0) * grad_scale)
    grad_queries = jnp.concatenate(dq_parts, axis=1)
    grad_keys = jnp.concatenate(dk_parts, axis=1)
    grad_values = jnp.concatenate(dv_parts, axis=1)
    grad_wv = jnp.concatenate(wv_parts, axis=1)
    return (grad_queries, grad_keys, grad_values, grad_wv)


def solution(mesh):
    devices = np.asarray(mesh.devices).reshape(-1)
    pair_mesh = Mesh(devices.reshape(-1, 2), DP)
    rows = P(DP, None)
    placed = (rows, rows, rows, rows, rows, P(), rows)
    return jax.shard_map(
        local,
        mesh=pair_mesh,
        in_specs=placed,
        out_specs=(rows, rows, rows, rows),
        check_vma=False,
    )
```

```python
import math

import jax
import jax.numpy as jnp
from jax import lax
from jax.sharding import Mesh, PartitionSpec as P
import numpy as np
from jax.experimental import pallas as pl
from jax.experimental.pallas import tpu as pltpu

HQ = 16
HK = 4
DH = 128
INTERPRET = False


NT = (((1,), (1,)), ((), ()))
TN = (((0,), (0,)), ((), ()))


def attend_kernel(
    seg_col_ref, seg_row_ref, key_col_ref, key_row_ref, q_ref, k_ref, v_ref, o_ref, out_ref
):
    row_count = q_ref.shape[0]
    group_size = HQ // HK
    q_w = group_size * DH
    score_scale = 1.0 / math.sqrt(DH)
    seg_row = seg_row_ref[...]
    live_queries = seg_row >= 0
    allowed = (
        (seg_col_ref[...] == seg_row) & (key_col_ref[...] <= key_row_ref[...]) & live_queries
    )
    k_group = k_ref[...]
    v_group = v_ref[...]
    dk_acc = jnp.zeros((row_count, DH), jnp.float32)
    dv_acc = jnp.zeros((row_count, DH), jnp.float32)
    for head in range(group_size):
        q_head = q_ref[:, head * DH : (head + 1) * DH]
        o_head = o_ref[:, head * DH : (head + 1) * DH]
        scores = lax.dot_general(k_group, q_head, NT, preferred_element_type=jnp.float32)
        scores = jnp.where(allowed, scores * score_scale, jnp.float32(-1000000000.0))
        col_max = jnp.max(scores, axis=0, keepdims=True)
        weights = jnp.exp(scores - col_max)
        scale_of = jnp.where(
            live_queries, 1.0 / jnp.sum(weights, axis=0, keepdims=True), jnp.float32(0.0)
        )
        attn_probs = weights * scale_of
        dv_acc = dv_acc + jnp.dot(
            attn_probs.astype(jnp.bfloat16), o_head, preferred_element_type=jnp.float32
        )
        dprob = lax.dot_general(v_group, o_head, NT, preferred_element_type=jnp.float32)
        row_delta = jnp.sum(attn_probs * dprob, axis=0, keepdims=True)
        dscore = (attn_probs * (dprob - row_delta) * score_scale).astype(jnp.bfloat16)
        out_ref[:, head * DH : (head + 1) * DH] = lax.dot_general(
            dscore, k_group, TN, preferred_element_type=jnp.float32
        ).astype(out_ref.dtype)
        dk_acc = dk_acc + jnp.dot(dscore, q_head, preferred_element_type=jnp.float32)
    out_ref[:, q_w : q_w + DH] = dk_acc.astype(out_ref.dtype)
    out_ref[:, q_w + DH : q_w + 2 * DH] = dv_acc.astype(out_ref.dtype)


def attend_rows(rows_in, segment, order_key, n_kv):
    row_count = rows_in.shape[0]
    q_w = (HQ // HK) * DH
    out_w = q_w + 2 * DH
    k_at, v_at, o_at = n_kv * q_w // DH, n_kv * q_w // DH + n_kv, (n_kv + 2 * n_kv * DH // q_w)
    whole = lambda g: (0, 0)
    col = pl.BlockSpec((row_count, 1), whole)
    row = pl.BlockSpec((1, row_count), whole)
    return pl.pallas_call(
        attend_kernel,
        grid=(n_kv,),
        in_specs=[
            col,
            row,
            col,
            row,
            pl.BlockSpec((row_count, q_w), lambda g: (0, g)),
            pl.BlockSpec((row_count, DH), lambda g: (0, k_at + g)),
            pl.BlockSpec((row_count, DH), lambda g: (0, v_at + g)),
            pl.BlockSpec((row_count, q_w), lambda g: (0, o_at + g)),
        ],
        out_specs=pl.BlockSpec((row_count, out_w), lambda g: (0, g)),
        out_shape=jax.ShapeDtypeStruct((row_count, n_kv * out_w), jnp.bfloat16),
        compiler_params=pltpu.CompilerParams(dimension_semantics=("arbitrary",)),
        interpret=INTERPRET,
    )(
        segment.reshape(row_count, 1),
        segment.reshape(1, row_count),
        order_key.reshape(row_count, 1),
        order_key.reshape(1, row_count),
        rows_in,
        rows_in,
        rows_in,
        rows_in,
    )


CHIP, CORE = "chip", "core"
DP = (CHIP, CORE)
PARTS = 2


def local(hidden_in, queries, keys, values, grad_attn, send_rows, slot_docs):
    chips, cores = lax.axis_size(CHIP), lax.axis_size(CORE)
    owners = chips * cores
    slot_count = send_rows.shape[0]
    tok_rows = queries.shape[0]
    group_size = HQ // HK
    q_w = group_size * DH
    live_send = (send_rows >= 0).T
    pick_rows = jnp.maximum(send_rows, 0).T
    grad_scale = 1.0 / math.sqrt(tok_rows * owners)
    row_ids = jnp.arange(owners * slot_count, dtype=jnp.int32)
    order_key = (row_ids % slot_count) * owners + row_ids // slot_count
    segment = jnp.tile(slot_docs[0].astype(jnp.int32), owners)
    targets = jnp.where(live_send, pick_rows, tok_rows).reshape(-1)
    out_w = q_w + 2 * DH
    core = lax.axis_index(CORE)
    swap = [(0, 1), (1, 0)]
    blocks = hidden_in.reshape(tok_rows, chips, cores, -1)
    mine = lax.dynamic_index_in_dim(blocks, core, axis=2, keepdims=False)
    theirs = lax.dynamic_index_in_dim(blocks, 1 - core, axis=2, keepdims=False)
    from_partner = lax.ppermute(theirs, CORE, swap)
    hidden_pair = jnp.concatenate((mine, from_partner), axis=0).reshape(2 * tok_rows, -1)
    n_kv = HK // PARTS
    dq_parts, dk_parts, dv_parts, wv_parts = [], [], [], []
    for part in range(PARTS):
        q_cols = slice(part * n_kv * q_w, (part + 1) * n_kv * q_w)
        kv_cols = slice(part * n_kv * DH, (part + 1) * n_kv * DH)
        table = jnp.concatenate(
            (queries[:, q_cols], keys[:, kv_cols], values[:, kv_cols], grad_attn[:, q_cols]), axis=1
        )
        rows_in = lax.all_to_all(table[pick_rows], DP, 0, 0, tiled=True)
        rows_in = rows_in.reshape(owners * slot_count, table.shape[1])
        rows_out = attend_rows(rows_in, segment, order_key, n_kv)
        back = lax.all_to_all(
            rows_out.reshape(owners, slot_count, rows_out.shape[1]), DP, 0, 0, tiled=True
        )
        home = (
            jnp.zeros((tok_rows, back.shape[2]), back.dtype)
            .at[targets]
            .set(back.reshape(owners * slot_count, back.shape[2]), mode="drop")
        )
        dq_parts += [home[:, g * out_w : g * out_w + q_w] for g in range(n_kv)]
        dk_parts += [home[:, g * out_w + q_w : g * out_w + q_w + DH] for g in range(n_kv)]
        dv_part = jnp.concatenate(
            [home[:, g * out_w + q_w + DH : (g + 1) * out_w] for g in range(n_kv)], axis=1
        )
        dv_parts.append(dv_part)
        grad_pair = jnp.concatenate((dv_part, lax.ppermute(dv_part, CORE, swap)), axis=0)
        partial = jnp.einsum(
            "td,tc->dc", hidden_pair, grad_pair, preferred_element_type=jnp.float32
        )
        wv_parts.append(partial.reshape(chips, partial.shape[0] // chips, partial.shape[1]))
    grad_queries = jnp.concatenate(dq_parts, axis=1)
    grad_keys = jnp.concatenate(dk_parts, axis=1)
    grad_values = jnp.concatenate(dv_parts, axis=1)
    partial = jnp.concatenate(wv_parts, axis=2)
    grad_wv = lax.all_to_all(partial, CHIP, 0, 0, tiled=True).sum(0) * grad_scale
    return (grad_queries, grad_keys, grad_values, grad_wv)


def solution(mesh):
    devices = np.asarray(mesh.devices).reshape(-1)
    pair_mesh = Mesh(devices.reshape(-1, 2), DP)
    rows = P(DP, None)
    placed = (rows, rows, rows, rows, rows, P(), rows)
    return jax.shard_map(
        local,
        mesh=pair_mesh,
        in_specs=placed,
        out_specs=(rows, rows, rows, rows),
        check_vma=False,
    )
```

```python
import math

import jax
import jax.numpy as jnp
from jax import lax
from jax.sharding import Mesh, PartitionSpec as P
import numpy as np
from jax.experimental import pallas as pl
from jax.experimental.pallas import tpu as pltpu

HQ = 16
HK = 4
DH = 128
INTERPRET = False


NT = (((1,), (1,)), ((), ()))
TN = (((0,), (0,)), ((), ()))


def attend_kernel(
    seg_col_ref, seg_row_ref, key_col_ref, key_row_ref, q_ref, k_ref, v_ref, o_ref, out_ref
):
    row_count = q_ref.shape[0]
    group_size = HQ // HK
    q_w = group_size * DH
    score_scale = 1.0 / math.sqrt(DH)
    seg_row = seg_row_ref[...]
    live_queries = seg_row >= 0
    allowed = (
        (seg_col_ref[...] == seg_row) & (key_col_ref[...] <= key_row_ref[...]) & live_queries
    )
    k_group = k_ref[...]
    v_group = v_ref[...]
    dk_acc = jnp.zeros((row_count, DH), jnp.float32)
    dv_acc = jnp.zeros((row_count, DH), jnp.float32)
    for head in range(group_size):
        q_head = q_ref[:, head * DH : (head + 1) * DH]
        o_head = o_ref[:, head * DH : (head + 1) * DH]
        scores = lax.dot_general(k_group, q_head, NT, preferred_element_type=jnp.float32)
        scores = jnp.where(allowed, scores * score_scale, jnp.float32(-1000000000.0))
        col_max = jnp.max(scores, axis=0, keepdims=True)
        weights = jnp.exp(scores - col_max)
        scale_of = jnp.where(
            live_queries, 1.0 / jnp.sum(weights, axis=0, keepdims=True), jnp.float32(0.0)
        )
        attn_probs = weights * scale_of
        dv_acc = dv_acc + jnp.dot(
            attn_probs.astype(jnp.bfloat16), o_head, preferred_element_type=jnp.float32
        )
        dprob = lax.dot_general(v_group, o_head, NT, preferred_element_type=jnp.float32)
        row_delta = jnp.sum(attn_probs * dprob, axis=0, keepdims=True)
        dscore = (attn_probs * (dprob - row_delta) * score_scale).astype(jnp.bfloat16)
        out_ref[:, head * DH : (head + 1) * DH] = lax.dot_general(
            dscore, k_group, TN, preferred_element_type=jnp.float32
        ).astype(out_ref.dtype)
        dk_acc = dk_acc + jnp.dot(dscore, q_head, preferred_element_type=jnp.float32)
    out_ref[:, q_w : q_w + DH] = dk_acc.astype(out_ref.dtype)
    out_ref[:, q_w + DH : q_w + 2 * DH] = dv_acc.astype(out_ref.dtype)


def attend_rows(rows_in, segment, order_key, n_kv):
    row_count = rows_in.shape[0]
    q_w = (HQ // HK) * DH
    out_w = q_w + 2 * DH
    o_at, k_at, v_at = n_kv, 2 * n_kv * q_w // DH, 2 * n_kv * q_w // DH + n_kv
    whole = lambda g: (0, 0)
    col = pl.BlockSpec((row_count, 1), whole)
    row = pl.BlockSpec((1, row_count), whole)
    return pl.pallas_call(
        attend_kernel,
        grid=(n_kv,),
        in_specs=[
            col,
            row,
            col,
            row,
            pl.BlockSpec((row_count, q_w), lambda g: (0, g)),
            pl.BlockSpec((row_count, DH), lambda g: (0, k_at + g)),
            pl.BlockSpec((row_count, DH), lambda g: (0, v_at + g)),
            pl.BlockSpec((row_count, q_w), lambda g: (0, o_at + g)),
        ],
        out_specs=pl.BlockSpec((row_count, out_w), lambda g: (0, g)),
        out_shape=jax.ShapeDtypeStruct((row_count, n_kv * out_w), jnp.bfloat16),
        compiler_params=pltpu.CompilerParams(dimension_semantics=("arbitrary",)),
        interpret=INTERPRET,
    )(
        segment.reshape(row_count, 1),
        segment.reshape(1, row_count),
        order_key.reshape(row_count, 1),
        order_key.reshape(1, row_count),
        rows_in,
        rows_in,
        rows_in,
        rows_in,
    )


CHIP, CORE = "chip", "core"
DP = (CHIP, CORE)
PARTS = ((0, 1), (1, HK - 1))


def local(hidden_in, queries, keys, values, grad_attn, send_rows, slot_docs):
    chips, cores = lax.axis_size(CHIP), lax.axis_size(CORE)
    owners = chips * cores
    slot_count = send_rows.shape[0]
    tok_rows = queries.shape[0]
    group_size = HQ // HK
    q_w = group_size * DH
    live_send = (send_rows >= 0).T
    pick_rows = jnp.maximum(send_rows, 0).T
    grad_scale = 1.0 / math.sqrt(tok_rows * owners)
    row_ids = jnp.arange(owners * slot_count, dtype=jnp.int32)
    order_key = (row_ids % slot_count) * owners + row_ids // slot_count
    segment = jnp.tile(slot_docs[0].astype(jnp.int32), owners)
    targets = jnp.where(live_send, pick_rows, tok_rows).reshape(-1)
    out_w = q_w + 2 * DH
    core = lax.axis_index(CORE)
    swap = [(0, 1), (1, 0)]
    blocks = hidden_in.reshape(tok_rows, chips, cores, -1)
    mine = lax.dynamic_index_in_dim(blocks, core, axis=2, keepdims=False)
    theirs = lax.dynamic_index_in_dim(blocks, 1 - core, axis=2, keepdims=False)
    from_partner = lax.ppermute(theirs, CORE, swap)
    hidden_pair = jnp.concatenate((mine, from_partner), axis=0).reshape(2 * tok_rows, -1)
    dq_parts, dk_parts, dv_parts, wv_parts = [], [], [], []
    for first, n_kv in PARTS:
        q_cols = slice(first * q_w, (first + n_kv) * q_w)
        kv_cols = slice(first * DH, (first + n_kv) * DH)
        table = jnp.concatenate(
            (queries[:, q_cols], grad_attn[:, q_cols], keys[:, kv_cols], values[:, kv_cols]), axis=1
        )
        rows_in = lax.all_to_all(table[pick_rows], DP, 0, 0, tiled=True)
        rows_in = rows_in.reshape(owners * slot_count, table.shape[1])
        rows_out = attend_rows(rows_in, segment, order_key, n_kv)
        back = lax.all_to_all(
            rows_out.reshape(owners, slot_count, rows_out.shape[1]), DP, 0, 0, tiled=True
        )
        home = (
            jnp.zeros((tok_rows, back.shape[2]), back.dtype)
            .at[targets]
            .set(back.reshape(owners * slot_count, back.shape[2]), mode="drop")
        )
        dq_parts += [home[:, g * out_w : g * out_w + q_w] for g in range(n_kv)]
        dk_parts += [home[:, g * out_w + q_w : g * out_w + q_w + DH] for g in range(n_kv)]
        dv_part = jnp.concatenate(
            [home[:, g * out_w + q_w + DH : (g + 1) * out_w] for g in range(n_kv)], axis=1
        )
        dv_parts.append(dv_part)
        grad_pair = jnp.concatenate((dv_part, lax.ppermute(dv_part, CORE, swap)), axis=0)
        partial = jnp.einsum(
            "td,tc->dc", hidden_pair, grad_pair, preferred_element_type=jnp.float32
        )
        partial = partial.reshape(chips, partial.shape[0] // chips, partial.shape[1])
        wv_parts.append(lax.all_to_all(partial, CHIP, 0, 0, tiled=True).sum(0) * grad_scale)
    grad_queries = jnp.concatenate(dq_parts, axis=1)
    grad_keys = jnp.concatenate(dk_parts, axis=1)
    grad_values = jnp.concatenate(dv_parts, axis=1)
    grad_wv = jnp.concatenate(wv_parts, axis=1)
    return (grad_queries, grad_keys, grad_values, grad_wv)


def solution(mesh):
    devices = np.asarray(mesh.devices).reshape(-1)
    pair_mesh = Mesh(devices.reshape(-1, 2), DP)
    rows = P(DP, None)
    placed = (rows, rows, rows, rows, rows, P(), rows)
    return jax.shard_map(
        local,
        mesh=pair_mesh,
        in_specs=placed,
        out_specs=(rows, rows, rows, rows),
        check_vma=False,
    )
```

```python
import math

import jax
import jax.numpy as jnp
from jax import lax
from jax.sharding import Mesh, PartitionSpec as P
import numpy as np
from jax.experimental import pallas as pl
from jax.experimental.pallas import tpu as pltpu

HQ = 16
HK = 4
DH = 128
INTERPRET = False


NT = (((1,), (1,)), ((), ()))
TN = (((0,), (0,)), ((), ()))


def attend_kernel(
    seg_col_ref, seg_row_ref, key_col_ref, key_row_ref, q_ref, k_ref, v_ref, o_ref, out_ref
):
    row_count = q_ref.shape[0]
    group_size = HQ // HK
    q_w = group_size * DH
    score_scale = 1.0 / math.sqrt(DH)
    seg_row = seg_row_ref[...]
    live_queries = seg_row >= 0
    allowed = (
        (seg_col_ref[...] == seg_row) & (key_col_ref[...] <= key_row_ref[...]) & live_queries
    )
    k_group = k_ref[...]
    v_group = v_ref[...]
    dk_acc = jnp.zeros((row_count, DH), jnp.float32)
    dv_acc = jnp.zeros((row_count, DH), jnp.float32)
    for head in range(group_size):
        q_head = q_ref[:, head * DH : (head + 1) * DH]
        o_head = o_ref[:, head * DH : (head + 1) * DH]
        scores = lax.dot_general(k_group, q_head, NT, preferred_element_type=jnp.float32)
        scores = jnp.where(allowed, scores * score_scale, jnp.float32(-1000000000.0))
        col_max = jnp.max(scores, axis=0, keepdims=True)
        weights = jnp.exp(scores - col_max)
        scale_of = jnp.where(
            live_queries, 1.0 / jnp.sum(weights, axis=0, keepdims=True), jnp.float32(0.0)
        )
        attn_probs = weights * scale_of
        dv_acc = dv_acc + jnp.dot(
            attn_probs.astype(jnp.bfloat16), o_head, preferred_element_type=jnp.float32
        )
        dprob = lax.dot_general(v_group, o_head, NT, preferred_element_type=jnp.float32)
        row_delta = jnp.sum(attn_probs * dprob, axis=0, keepdims=True)
        dscore = (attn_probs * (dprob - row_delta) * score_scale).astype(jnp.bfloat16)
        out_ref[:, head * DH : (head + 1) * DH] = lax.dot_general(
            dscore, k_group, TN, preferred_element_type=jnp.float32
        ).astype(out_ref.dtype)
        dk_acc = dk_acc + jnp.dot(dscore, q_head, preferred_element_type=jnp.float32)
    out_ref[:, q_w : q_w + DH] = dk_acc.astype(out_ref.dtype)
    out_ref[:, q_w + DH : q_w + 2 * DH] = dv_acc.astype(out_ref.dtype)


def attend_rows(rows_in, segment, order_key, n_kv):
    row_count = rows_in.shape[0]
    q_w = (HQ // HK) * DH
    out_w = q_w + 2 * DH
    o_at, k_at, v_at = n_kv, 2 * n_kv * q_w // DH, 2 * n_kv * q_w // DH + n_kv
    whole = lambda g: (0, 0)
    col = pl.BlockSpec((row_count, 1), whole)
    row = pl.BlockSpec((1, row_count), whole)
    return pl.pallas_call(
        attend_kernel,
        grid=(n_kv,),
        in_specs=[
            col,
            row,
            col,
            row,
            pl.BlockSpec((row_count, q_w), lambda g: (0, g)),
            pl.BlockSpec((row_count, DH), lambda g: (0, k_at + g)),
            pl.BlockSpec((row_count, DH), lambda g: (0, v_at + g)),
            pl.BlockSpec((row_count, q_w), lambda g: (0, o_at + g)),
        ],
        out_specs=pl.BlockSpec((row_count, out_w), lambda g: (0, g)),
        out_shape=jax.ShapeDtypeStruct((row_count, n_kv * out_w), jnp.bfloat16),
        compiler_params=pltpu.CompilerParams(dimension_semantics=("arbitrary",)),
        interpret=INTERPRET,
    )(
        segment.reshape(row_count, 1),
        segment.reshape(1, row_count),
        order_key.reshape(row_count, 1),
        order_key.reshape(1, row_count),
        rows_in,
        rows_in,
        rows_in,
        rows_in,
    )


CHIP, CORE = "chip", "core"
DP = (CHIP, CORE)
PARTS = ((0, HK - 1), (HK - 1, 1))


def local(hidden_in, queries, keys, values, grad_attn, send_rows, slot_docs):
    chips, cores = lax.axis_size(CHIP), lax.axis_size(CORE)
    owners = chips * cores
    slot_count = send_rows.shape[0]
    tok_rows = queries.shape[0]
    group_size = HQ // HK
    q_w = group_size * DH
    live_send = (send_rows >= 0).T
    pick_rows = jnp.maximum(send_rows, 0).T
    grad_scale = 1.0 / math.sqrt(tok_rows * owners)
    row_ids = jnp.arange(owners * slot_count, dtype=jnp.int32)
    order_key = (row_ids % slot_count) * owners + row_ids // slot_count
    segment = jnp.tile(slot_docs[0].astype(jnp.int32), owners)
    targets = jnp.where(live_send, pick_rows, tok_rows).reshape(-1)
    out_w = q_w + 2 * DH
    core = lax.axis_index(CORE)
    swap = [(0, 1), (1, 0)]
    blocks = hidden_in.reshape(tok_rows, chips, cores, -1)
    mine = lax.dynamic_index_in_dim(blocks, core, axis=2, keepdims=False)
    theirs = lax.dynamic_index_in_dim(blocks, 1 - core, axis=2, keepdims=False)
    from_partner = lax.ppermute(theirs, CORE, swap)
    hidden_pair = jnp.concatenate((mine, from_partner), axis=0).reshape(2 * tok_rows, -1)
    dq_parts, dk_parts, dv_parts, wv_parts = [], [], [], []
    for first, n_kv in PARTS:
        q_cols = slice(first * q_w, (first + n_kv) * q_w)
        kv_cols = slice(first * DH, (first + n_kv) * DH)
        table = jnp.concatenate(
            (queries[:, q_cols], grad_attn[:, q_cols], keys[:, kv_cols], values[:, kv_cols]), axis=1
        )
        rows_in = lax.all_to_all(table[pick_rows], DP, 0, 0, tiled=True)
        rows_in = rows_in.reshape(owners * slot_count, table.shape[1])
        rows_out = attend_rows(rows_in, segment, order_key, n_kv)
        back = lax.all_to_all(
            rows_out.reshape(owners, slot_count, rows_out.shape[1]), DP, 0, 0, tiled=True
        )
        home = (
            jnp.zeros((tok_rows, back.shape[2]), back.dtype)
            .at[targets]
            .set(back.reshape(owners * slot_count, back.shape[2]), mode="drop")
        )
        dq_parts += [home[:, g * out_w : g * out_w + q_w] for g in range(n_kv)]
        dk_parts += [home[:, g * out_w + q_w : g * out_w + q_w + DH] for g in range(n_kv)]
        dv_part = jnp.concatenate(
            [home[:, g * out_w + q_w + DH : (g + 1) * out_w] for g in range(n_kv)], axis=1
        )
        dv_parts.append(dv_part)
        grad_pair = jnp.concatenate((dv_part, lax.ppermute(dv_part, CORE, swap)), axis=0)
        partial = jnp.einsum(
            "td,tc->dc", hidden_pair, grad_pair, preferred_element_type=jnp.float32
        )
        partial = partial.reshape(chips, partial.shape[0] // chips, partial.shape[1])
        wv_parts.append(lax.all_to_all(partial, CHIP, 0, 0, tiled=True).sum(0) * grad_scale)
    grad_queries = jnp.concatenate(dq_parts, axis=1)
    grad_keys = jnp.concatenate(dk_parts, axis=1)
    grad_values = jnp.concatenate(dv_parts, axis=1)
    grad_wv = jnp.concatenate(wv_parts, axis=1)
    return (grad_queries, grad_keys, grad_values, grad_wv)


def solution(mesh):
    devices = np.asarray(mesh.devices).reshape(-1)
    pair_mesh = Mesh(devices.reshape(-1, 2), DP)
    rows = P(DP, None)
    placed = (rows, rows, rows, rows, rows, P(), rows)
    return jax.shard_map(
        local,
        mesh=pair_mesh,
        in_specs=placed,
        out_specs=(rows, rows, rows, rows),
        check_vma=False,
    )
```
